256 devices in a mesh: tm: 8 (over z), space: 16 (over y, x), branch: 2 (over core).
Axes of the slice: x: 4, y: 4, z: 8, core: 2. Of those that a mesh axis runs over, the one named last changes fastest.
Arguments:
- state: float32 [2, 8, 2, 256, 1024], P('branch', 'tm', None, 'space'), may hold values from -13 to 15
- panel: float32 [2, 8, 16, 2, 256, 1024], P('branch', 'tm', None, None, 'space'), may hold values from -4 to 4
- region: int32 [256, 1024], P('space'), may hold values from 0 to 5
- feed_table: float32 [6], replicated, may hold values from 0.5 to 2.5
- step_counts: int32 [8], P('tm'), may hold values from 2 to 5, as said below
Outputs:
- deflated: float32 [2, 8, 2, 256, 1024], P('branch', 'tm', None, 'space')
- correction: float32 [2, 8, 2, 256, 1024], P('branch', 'tm', None, 'space')
- coefficients: float32 [2, 16], P('branch')
The draws below stay inside these ranges and needn't reach their ends.
Inputs may be any that keep to these rules, and one draw needn't show every extreme that they name: `step_counts`: some segment takes 5 steps.
All inputs are finite; a program needn't handle non-finite values.
Results may differ from the reference program's by a relative error of at most 0.0003.
Values sent between devices are 32-bit elements; how exact they have to be, the bound alone decides.
No kernel may reach another device: no remote copies, remote signals or barrier semaphores. Data moves between devices by JAX's collectives and lax.ppermute only.
A program may use at most 64 MiB of HBM per device.

```python
import math
import jax
import jax.numpy as jnp
from jax import lax

COLS = 1024
STEPS = 5
DIRECTIONS = 16
CLASSES = 6
SEGS = 8
BRANCHES = 2
ROWS = 256


def joint_draw(key):
    panel_shape = (BRANCHES, SEGS, DIRECTIONS, 2, ROWS, COLS)
    column_shape = (BRANCHES, SEGS, DIRECTIONS, 1, 1, 1)
    panel_key = jax.random.fold_in(key, 101)
    directions = jax.random.truncated_normal(panel_key, -4.0, 4.0, panel_shape)
    baseline = jax.random.uniform(jax.random.fold_in(key, 103), (BRANCHES, SEGS, 2, ROWS, COLS), minval=0.8, maxval=1.8)
    mixing = jax.random.uniform(jax.random.fold_in(key, 104), column_shape, minval=-0.2, maxval=0.2)
    start = baseline + jnp.sum(mixing * directions, axis=2)
    return (start.astype(jnp.float32), directions.astype(jnp.float32))


def draw_state(key, part):
    return joint_draw(key)[0]


def draw_panel(key, part):
    return joint_draw(key)[1]


def draw_step_counts(key, part):
    limits = jax.random.randint(jax.random.fold_in(key, 201), (SEGS,), STEPS // 2, STEPS + 1)
    chosen = jax.random.randint(jax.random.fold_in(key, 202), (), 0, SEGS)
    return jnp.where(jnp.arange(SEGS) == chosen, STEPS, limits).astype(jnp.int32)


def place_ends(values, stream_key, low, largest):
    index_at = [jax.random.randint(jax.random.fold_in(stream_key, axis), (), 0, length) for axis, length in enumerate(values.shape)]
    longest = values.shape.index(max(values.shape))
    neighbour = index_at[:longest] + [(index_at[longest] + 1) % values.shape[longest]] + index_at[longest + 1:]
    return values.at[tuple(index_at)].set(low).at[tuple(neighbour)].set(largest)


def setup_inputs(seed: int = 0) -> dict:
    seeds = jax.random.split(jax.random.key(seed), 6)
    return {
        "state": draw_state(jax.random.fold_in(seeds[5], 71), 0),
        "panel": draw_panel(jax.random.fold_in(seeds[5], 71), 0),
        "region": place_ends(jax.random.randint(seeds[2], (ROWS, COLS), 0, CLASSES), jax.random.fold_in(seeds[2], 1), 0, CLASSES - 1).astype(jnp.int32),
        "feed_table": jnp.clip(jnp.exp(jax.random.uniform(seeds[3], (CLASSES,), jnp.float32, math.log(0.5), math.log(2.5))), 0.5, 2.5),
        "step_counts": draw_step_counts(jax.random.fold_in(seeds[5], 71), 0),
    }


TIME_STEP = 0.03
ACTIVATOR_DIFFUSION = 1.0
INHIBITOR_DIFFUSION = 6.0
REACTION_RATE = 2.5
SMALL_EPSILON = 1e-06
HIGHEST = lax.Precision.HIGHEST

def laplacian_rows(extended):
    interior = extended[:, 1:-1, :]
    return extended[:, 2:, :] + extended[:, :-2, :] + jnp.roll(interior, 1, 2) + jnp.roll(interior, -1, 2) - 4.0 * interior

def advance(extended, feed_rate, active):
    laplacian = laplacian_rows(extended)
    interior = extended[:, 1:-1, :]
    activator = interior[0]
    inhibitor = interior[1]
    squared = activator * activator
    product = activator * inhibitor
    new_activator = activator + TIME_STEP * (ACTIVATOR_DIFFUSION * laplacian[0] + feed_rate - (REACTION_RATE + 1.0) * activator + squared * inhibitor)
    new_inhibitor = inhibitor + TIME_STEP * (INHIBITOR_DIFFUSION * laplacian[1] + REACTION_RATE * activator - squared * inhibitor)
    tangent_act = interior[2::2]
    tangent_inh = interior[3::2]
    new_tangent_act = tangent_act + TIME_STEP * (ACTIVATOR_DIFFUSION * laplacian[2::2] + (2.0 * product - REACTION_RATE - 1.0) * tangent_act + squared * tangent_inh)
    new_tangent_inh = tangent_inh + TIME_STEP * (INHIBITOR_DIFFUSION * laplacian[3::2] + (REACTION_RATE - 2.0 * product) * tangent_act - squared * tangent_inh)
    tangents = jnp.stack([new_tangent_act, new_tangent_inh], 1).reshape(tangent_act.shape[0] * 2, activator.shape[0], activator.shape[1])
    advanced = jnp.concatenate([new_activator[None], new_inhibitor[None], tangents], 0)
    return jnp.where(active, advanced, interior)

def solve_small(gram, rhs):
    size = gram.shape[0]
    index = jnp.arange(size)
    columns = []
    pivots = []
    for outer in range(size):
        value = gram[:, outer]
        for inner in range(outer):
            value = value - columns[inner] * columns[inner][outer]
        pivot = jnp.sqrt(value[outer])
        columns.append(jnp.where(index >= outer, value / pivot, jnp.zeros_like(value)))
        pivots.append(pivot)
    middle = []
    for outer in range(size):
        accum = -rhs[outer]
        for inner in range(outer):
            accum = accum - columns[inner][outer] * middle[inner]
        middle.append(accum / pivots[outer])
    result = [None] * size
    for outer in range(size - 1, -1, -1):
        accum = middle[outer]
        for inner in range(outer + 1, size):
            accum = accum - columns[outer][inner] * result[inner]
        result[outer] = accum / pivots[outer]
    return jnp.stack(result, 0)

def reference(state, panel, region, feed_table, step_counts):
    feed_rate = jnp.take(feed_table, region, axis=0)
    branches, segments, fields, row_count, column_count = state.shape
    directions = panel.shape[2]
    channels = fields + 2 * directions
    flat_state = state.reshape(branches * segments, fields, row_count, column_count)
    flat_panel = panel.reshape(branches * segments, 2 * directions, row_count, column_count)
    limits = jnp.tile(step_counts, branches)

    def propagate(segment_item):
        start, tangent, step_limit = segment_item
        stacked = jnp.concatenate([start, tangent], 0)
        for step_index in range(STEPS):
            extended = jnp.concatenate([stacked[:, -1:], stacked, stacked[:, :1]], 1)
            stacked = advance(extended, feed_rate, step_index < step_limit)
        return stacked
    ends = lax.map(propagate, (flat_state, flat_panel, limits)).reshape(branches, segments, channels, row_count, column_count)
    arrived = jnp.roll(ends, 1, axis=1)
    mismatch = (arrived[:, :, :2] - state).reshape(branches, segments, -1)
    panel_rows = panel.reshape(branches, segments, directions, -1)
    jacobian_panel = arrived[:, :, 2:].reshape(branches, segments, directions, -1) - panel_rows
    total = 2.0 * segments * row_count * column_count
    separation = (state - state[::-1]).reshape(branches, segments, -1)
    deflated_all = []
    correction_all = []
    coefficient_all = []
    for branch_index in range(branches):
        gap = separation[branch_index]
        distance = jnp.sum(gap * gap) / total + SMALL_EPSILON
        along = jnp.einsum('sjn,sn->j', panel_rows[branch_index], gap, precision=HIGHEST) / total
        deflator = 1.0 / distance + 1.0
        slopes = -2.0 * along / (distance * distance)
        deflated = deflator * mismatch[branch_index]
        deflated_panel = deflator * jacobian_panel[branch_index] + slopes[None, :, None] * mismatch[branch_index][:, None, :]
        gram = jnp.einsum('sjn,skn->jk', deflated_panel, deflated_panel, precision=HIGHEST) / total
        rhs = jnp.einsum('sjn,sn->j', deflated_panel, deflated, precision=HIGHEST) / total
        coefficients = solve_small(gram, rhs)
        correction = jnp.einsum('j,sjn->sn', coefficients, panel_rows[branch_index], precision=HIGHEST)
        deflated_all.append(deflated.reshape(segments, fields, row_count, column_count))
        correction_all.append(correction.reshape(segments, fields, row_count, column_count))
        coefficient_all.append(coefficients)
    return (jnp.stack(deflated_all, 0), jnp.stack(correction_all, 0), jnp.stack(coefficient_all, 0))
```

```python
import functools

import jax
import jax.numpy as jnp
from jax import lax
from jax.sharding import Mesh
from jax.sharding import PartitionSpec as P
from jax.experimental import pallas as pl

STEPS = 5
SPACE = ("space_0", "space_1")
TM_SPACE = ("tm", "space_0", "space_1")


TIME_STEP = 0.03
ACTIVATOR_DIFFUSION = 1.0
INHIBITOR_DIFFUSION = 6.0
REACTION_RATE = 2.5
SMALL_EPSILON = 1e-06
HIGHEST = lax.Precision.HIGHEST


def extended_2(cells, sides, width):
    for axis, dim in sides:
        count = lax.axis_size(axis)
        head = lax.slice_in_dim(cells, 0, width, axis=dim)
        tail = lax.slice_in_dim(cells, cells.shape[dim] - width, cells.shape[dim], axis=dim)
        cells = jnp.concatenate(
            [
                lax.ppermute(tail, axis, [(i, (i + 1) % count) for i in range(count)]),
                cells,
                lax.ppermute(head, axis, [((i + 1) % count, i) for i in range(count)]),
            ],
            axis=dim,
        )
    return cells


def swapped(value, axis, apart):
    mask = 2**apart
    pairs = [(source, source ^ mask) for source in range(lax.axis_size(axis))]
    return lax.ppermute(value, axis, pairs)


def passed_along(block, axis, distance):
    devices = range(lax.axis_size(axis))
    route = [((i - distance) % len(devices), i) for i in devices]
    return lax.ppermute(block, axis, route)


def one_axis_at_a_time(x, axes):
    return functools.reduce(lax.psum, axes, x)


def laplacian_rows(extended):
    interior = extended[:, 1:-1, :]
    return (
        extended[:, 2:, :]
        + extended[:, :-2, :]
        + jnp.roll(interior, 1, 2)
        + jnp.roll(interior, -1, 2)
        - 4.0 * interior
    )


def advance(extended, feed_rate, active):
    laplacian = laplacian_rows(extended)
    interior = extended[:, 1:-1, :]
    activator = interior[0]
    inhibitor = interior[1]
    squared = activator * activator
    product = activator * inhibitor
    new_activator = activator + TIME_STEP * (
        ACTIVATOR_DIFFUSION * laplacian[0]
        + feed_rate
        - (REACTION_RATE + 1.0) * activator
        + squared * inhibitor
    )
    new_inhibitor = inhibitor + TIME_STEP * (
        INHIBITOR_DIFFUSION * laplacian[1] + REACTION_RATE * activator - squared * inhibitor
    )
    tangent_act = interior[2::2]
    tangent_inh = interior[3::2]
    new_tangent_act = tangent_act + TIME_STEP * (
        ACTIVATOR_DIFFUSION * laplacian[2::2]
        + (2.0 * product - REACTION_RATE - 1.0) * tangent_act
        + squared * tangent_inh
    )
    new_tangent_inh = tangent_inh + TIME_STEP * (
        INHIBITOR_DIFFUSION * laplacian[3::2]
        + (REACTION_RATE - 2.0 * product) * tangent_act
        - squared * tangent_inh
    )
    tangents = jnp.stack([new_tangent_act, new_tangent_inh], 1).reshape(
        tangent_act.shape[0] * 2, activator.shape[0], activator.shape[1]
    )
    advanced = jnp.concatenate([new_activator[None], new_inhibitor[None], tangents], 0)
    return jnp.where(active, advanced, interior)


def cholesky_kernel(gram_ref, rhs_ref, out_ref):
    size = gram_ref.shape[0]
    tile = gram_ref[...]
    rows = lax.broadcasted_iota(jnp.int32, tile.shape, 0)
    cols = lax.broadcasted_iota(jnp.int32, tile.shape, 1)
    diagonal = rows == cols
    index = rows[:, :1]
    columns = []
    pivots = []
    for outer in range(size):
        value = jnp.sum(jnp.where(cols == outer, tile, 0.0), axis=1, keepdims=True)
        pivot = jnp.sqrt(jnp.sum(jnp.where(index == outer, value, 0.0), axis=0, keepdims=True))
        column = jnp.where(index >= outer, value / pivot, 0.0)
        row = jnp.sum(jnp.where(diagonal, column, 0.0), axis=0, keepdims=True)
        tile = tile - column * row
        columns.append(column)
        pivots.append(pivot)
    accum = -jnp.sum(jnp.where(diagonal, rhs_ref[...], 0.0), axis=1, keepdims=True)
    middle = jnp.zeros_like(accum)
    for outer in range(size):
        value = jnp.sum(jnp.where(index == outer, accum, 0.0), axis=0, keepdims=True) / pivots[outer]
        middle = jnp.where(index == outer, value, middle)
        accum = accum - columns[outer] * value
    result = jnp.zeros_like(middle)
    for outer in range(size - 1, -1, -1):
        below = jnp.sum(jnp.where(index > outer, columns[outer] * result, 0.0), axis=0, keepdims=True)
        value = jnp.sum(jnp.where(index == outer, middle, 0.0), axis=0, keepdims=True)
        result = jnp.where(index == outer, (value - below) / pivots[outer], result)
    out_ref[...] = jnp.sum(jnp.where(diagonal, result, 0.0), axis=0, keepdims=True)


def solve_small(gram, rhs):
    size = gram.shape[0]
    lanes = 128
    padded = jnp.pad(gram, ((0, 0), (0, lanes - size)))
    rhs_row = jnp.pad(rhs, (0, lanes - size)).reshape(1, lanes)
    out = pl.pallas_call(
        cholesky_kernel, out_shape=jax.ShapeDtypeStruct((1, lanes), jnp.float32)
    )(padded, rhs_row)
    return out[0, :size]


def on_device(state, panel, region, feed_table, step_counts):
    start = state[0, 0]
    row_count = start.shape[1]
    column_count = start.shape[2]
    directions = panel.shape[2]
    tangent = panel[0, 0].reshape(2 * directions, row_count, column_count)
    stacked = jnp.concatenate([start, tangent], 0)
    following = passed_along(stacked, "tm", -1)
    partner_state = swapped(start, "branch", 0)
    classes = jnp.arange(feed_table.shape[0], dtype=jnp.int32)
    feed_rate = jnp.sum(
        jnp.where(region[None] == classes[:, None, None], feed_table[:, None, None], 0.0), 0
    )
    step_limit = step_counts[0]
    panel_rows = panel[0, 0].reshape(directions, -1)
    gap = (start - partner_state).reshape(-1)
    total = 2.0 * lax.axis_size("tm") * row_count * lax.axis_size(SPACE) * column_count
    gap_part = jnp.sum(gap * gap)
    along_part = jnp.dot(panel_rows, gap, precision=HIGHEST)
    first_sum = lax.psum(jnp.concatenate([gap_part[None], along_part]), TM_SPACE)
    gap_sum = first_sum[0]
    along_sum = first_sum[1:]
    widened = extended_2(jnp.concatenate([stacked, feed_rate[None]], 0), ((SPACE, 1),), STEPS)
    stacked = widened[:-1]
    feed_wide = widened[-1]
    total_rows = feed_wide.shape[0]
    for step_index in range(STEPS):
        stacked = advance(
            stacked,
            feed_wide[step_index + 1 : total_rows - step_index - 1],
            step_index < step_limit,
        )
    arrived = passed_along(stacked[:2], "tm", 1)
    mismatch = (arrived - start).reshape(-1)
    next_mismatch = (stacked[:2] - following[:2]).reshape(-1)
    next_jacobian = stacked[2:].reshape(directions, -1) - following[2:].reshape(directions, -1)
    distance = gap_sum / total + SMALL_EPSILON
    deflator = 1.0 / distance + 1.0
    slopes = -2.0 * (along_sum / total) / (distance * distance)
    deflated = deflator * mismatch
    next_deflated = deflator * next_mismatch
    deflated_panel = deflator * next_jacobian + slopes[:, None] * next_mismatch[None, :]
    gram_part = jnp.dot(deflated_panel, deflated_panel.T, precision=HIGHEST)
    rhs_part = jnp.dot(deflated_panel, next_deflated, precision=HIGHEST)
    second_sum = lax.psum(
        jnp.concatenate([gram_part.reshape(-1), rhs_part]), TM_SPACE
    )
    gram = second_sum[: directions * directions].reshape(directions, directions) / total
    rhs = second_sum[directions * directions :] / total
    coefficients = solve_small(gram, rhs)
    correction = jnp.dot(coefficients, panel_rows, precision=HIGHEST)
    return (
        deflated.reshape(1, 1, 2, row_count, column_count),
        correction.reshape(1, 1, 2, row_count, column_count),
        coefficients.reshape(1, directions),
    )


def solution(mesh):
    finer = Mesh(
        mesh.devices.reshape(mesh.shape["tm"], 4, 4, mesh.shape["branch"]),
        ("tm", "space_0", "space_1", "branch"),
    )
    in_specs = (
        P("branch", "tm", None, SPACE, None),
        P("branch", "tm", None, None, SPACE, None),
        P(SPACE, None),
        P(),
        P("tm"),
    )
    out_specs = (
        P("branch", "tm", None, SPACE, None),
        P("branch", "tm", None, SPACE, None),
        P("branch", None),
    )
    return jax.shard_map(
        on_device, mesh=finer, in_specs=in_specs, out_specs=out_specs, check_vma=False
    )
```

```python
import jax
import jax.numpy as jnp
from jax import lax
from jax.sharding import Mesh
from jax.sharding import PartitionSpec as P
from jax.experimental import pallas as pl

STEPS = 5
SPACE = ("space_0", "space_1")
TM_SPACE = ("tm", "space_0", "space_1")


TIME_STEP = 0.03
ACTIVATOR_DIFFUSION = 1.0
INHIBITOR_DIFFUSION = 6.0
REACTION_RATE = 2.5
SMALL_EPSILON = 1e-06
HIGHEST = lax.Precision.HIGHEST


def extended_2(cells, sides, width):
    for axis, dim in sides:
        count = lax.axis_size(axis)
        head = lax.slice_in_dim(cells, 0, width, axis=dim)
        tail = lax.slice_in_dim(cells, cells.shape[dim] - width, cells.shape[dim], axis=dim)
        cells = jnp.concatenate(
            [
                lax.ppermute(tail, axis, [(i, (i + 1) % count) for i in range(count)]),
                cells,
                lax.ppermute(head, axis, [((i + 1) % count, i) for i in range(count)]),
            ],
            axis=dim,
        )
    return cells


def swapped(value, axis, apart):
    mask = 2**apart
    pairs = [(source, source ^ mask) for source in range(lax.axis_size(axis))]
    return lax.ppermute(value, axis, pairs)


def passed_along(block, axis, distance):
    devices = range(lax.axis_size(axis))
    route = [((i - distance) % len(devices), i) for i in devices]
    return lax.ppermute(block, axis, route)


def butterfly_rounds(axes):
    rounds = []
    for axis in axes:
        count = lax.axis_size(axis)
        apart = 1
        while apart < count:
            rounds.append((axis, [(i, i ^ apart) for i in range(count)]))
            apart *= 2
    return rounds


def one_axis_at_a_time(x, axes):
    for axis, pairs in butterfly_rounds(axes):
        x = x + lax.ppermute(x, axis, pairs)
    return x


def laplacian_rows(extended):
    interior = extended[:, 1:-1, :]
    return (
        extended[:, 2:, :]
        + extended[:, :-2, :]
        + jnp.roll(interior, 1, 2)
        + jnp.roll(interior, -1, 2)
        - 4.0 * interior
    )


def advance(extended, feed_rate, active):
    laplacian = laplacian_rows(extended)
    interior = extended[:, 1:-1, :]
    activator = interior[0]
    inhibitor = interior[1]
    squared = activator * activator
    product = activator * inhibitor
    new_activator = activator + TIME_STEP * (
        ACTIVATOR_DIFFUSION * laplacian[0]
        + feed_rate
        - (REACTION_RATE + 1.0) * activator
        + squared * inhibitor
    )
    new_inhibitor = inhibitor + TIME_STEP * (
        INHIBITOR_DIFFUSION * laplacian[1] + REACTION_RATE * activator - squared * inhibitor
    )
    tangent_act = interior[2::2]
    tangent_inh = interior[3::2]
    new_tangent_act = tangent_act + TIME_STEP * (
        ACTIVATOR_DIFFUSION * laplacian[2::2]
        + (2.0 * product - REACTION_RATE - 1.0) * tangent_act
        + squared * tangent_inh
    )
    new_tangent_inh = tangent_inh + TIME_STEP * (
        INHIBITOR_DIFFUSION * laplacian[3::2]
        + (REACTION_RATE - 2.0 * product) * tangent_act
        - squared * tangent_inh
    )
    tangents = jnp.stack([new_tangent_act, new_tangent_inh], 1).reshape(
        tangent_act.shape[0] * 2, activator.shape[0], activator.shape[1]
    )
    advanced = jnp.concatenate([new_activator[None], new_inhibitor[None], tangents], 0)
    return jnp.where(active, advanced, interior)


def cholesky_kernel(gram_ref, rhs_ref, out_ref):
    size = gram_ref.shape[0]
    tile = gram_ref[...]
    rows = lax.broadcasted_iota(jnp.int32, tile.shape, 0)
    cols = lax.broadcasted_iota(jnp.int32, tile.shape, 1)
    diagonal = rows == cols
    index = rows[:, :1]
    columns = []
    pivots = []
    for outer in range(size):
        value = jnp.sum(jnp.where(cols == outer, tile, 0.0), axis=1, keepdims=True)
        pivot = jnp.sqrt(jnp.sum(jnp.where(index == outer, value, 0.0), axis=0, keepdims=True))
        column = jnp.where(index >= outer, value / pivot, 0.0)
        row = jnp.sum(jnp.where(diagonal, column, 0.0), axis=0, keepdims=True)
        tile = tile - column * row
        columns.append(column)
        pivots.append(pivot)
    accum = -jnp.sum(jnp.where(diagonal, rhs_ref[...], 0.0), axis=1, keepdims=True)
    middle = jnp.zeros_like(accum)
    for outer in range(size):
        value = jnp.sum(jnp.where(index == outer, accum, 0.0), axis=0, keepdims=True) / pivots[outer]
        middle = jnp.where(index == outer, value, middle)
        accum = accum - columns[outer] * value
    result = jnp.zeros_like(middle)
    for outer in range(size - 1, -1, -1):
        below = jnp.sum(jnp.where(index > outer, columns[outer] * result, 0.0), axis=0, keepdims=True)
        value = jnp.sum(jnp.where(index == outer, middle, 0.0), axis=0, keepdims=True)
        result = jnp.where(index == outer, (value - below) / pivots[outer], result)
    out_ref[...] = jnp.sum(jnp.where(diagonal, result, 0.0), axis=0, keepdims=True)


def solve_small(gram, rhs):
    size = gram.shape[0]
    lanes = 128
    padded = jnp.pad(gram, ((0, 0), (0, lanes - size)))
    rhs_row = jnp.pad(rhs, (0, lanes - size)).reshape(1, lanes)
    out = pl.pallas_call(
        cholesky_kernel, out_shape=jax.ShapeDtypeStruct((1, lanes), jnp.float32)
    )(padded, rhs_row)
    return out[0, :size]


def on_device(state, panel, region, feed_table, step_counts):
    start = state[0, 0]
    row_count = start.shape[1]
    column_count = start.shape[2]
    directions = panel.shape[2]
    tangent = panel[0, 0].reshape(2 * directions, row_count, column_count)
    stacked = jnp.concatenate([start, tangent], 0)
    following = passed_along(stacked, "tm", -1)
    partner_state = swapped(start, "branch", 0)
    classes = jnp.arange(feed_table.shape[0], dtype=jnp.int32)
    feed_rate = jnp.sum(
        jnp.where(region[None] == classes[:, None, None], feed_table[:, None, None], 0.0), 0
    )
    step_limit = step_counts[0]
    panel_rows = panel[0, 0].reshape(directions, -1)
    gap = (start - partner_state).reshape(-1)
    total = 2.0 * lax.axis_size("tm") * row_count * lax.axis_size(SPACE) * column_count
    gap_part = jnp.sum(gap * gap)
    along_part = jnp.dot(panel_rows, gap, precision=HIGHEST)
    first_sum = jnp.concatenate([gap_part[None], along_part])
    widened = extended_2(jnp.concatenate([stacked, feed_rate[None]], 0), ((SPACE, 1),), STEPS)
    stacked = widened[:-1]
    feed_wide = widened[-1]
    total_rows = feed_wide.shape[0]
    rounds = butterfly_rounds(TM_SPACE)
    per_step = -(-len(rounds) // STEPS)
    for step_index in range(STEPS):
        stacked = advance(
            stacked,
            feed_wide[step_index + 1 : total_rows - step_index - 1],
            step_index < step_limit,
        )
        for axis, pairs in rounds[:per_step]:
            first_sum = first_sum + lax.ppermute(first_sum, axis, pairs)
        rounds = rounds[per_step:]
        stacked, first_sum = lax.optimization_barrier((stacked, first_sum))
    for axis, pairs in rounds:
        first_sum = first_sum + lax.ppermute(first_sum, axis, pairs)
    gap_sum = first_sum[0]
    along_sum = first_sum[1:]
    arrived = passed_along(stacked[:2], "tm", 1)
    mismatch = (arrived - start).reshape(-1)
    next_mismatch = (stacked[:2] - following[:2]).reshape(-1)
    next_jacobian = stacked[2:].reshape(directions, -1) - following[2:].reshape(directions, -1)
    distance = gap_sum / total + SMALL_EPSILON
    deflator = 1.0 / distance + 1.0
    slopes = -2.0 * (along_sum / total) / (distance * distance)
    deflated = deflator * mismatch
    next_deflated = deflator * next_mismatch
    deflated_panel = deflator * next_jacobian + slopes[:, None] * next_mismatch[None, :]
    gram_part = jnp.dot(deflated_panel, deflated_panel.T, precision=HIGHEST)
    rhs_part = jnp.dot(deflated_panel, next_deflated, precision=HIGHEST)
    second_sum = one_axis_at_a_time(
        jnp.concatenate([gram_part.reshape(-1), rhs_part]), TM_SPACE
    )
    gram = second_sum[: directions * directions].reshape(directions, directions) / total
    rhs = second_sum[directions * directions :] / total
    coefficients = solve_small(gram, rhs)
    correction = jnp.dot(coefficients, panel_rows, precision=HIGHEST)
    return (
        deflated.reshape(1, 1, 2, row_count, column_count),
        correction.reshape(1, 1, 2, row_count, column_count),
        coefficients.reshape(1, directions),
    )


def solution(mesh):
    finer = Mesh(
        mesh.devices.reshape(mesh.shape["tm"], 4, 4, mesh.shape["branch"]),
        ("tm", "space_0", "space_1", "branch"),
    )
    in_specs = (
        P("branch", "tm", None, SPACE, None),
        P("branch", "tm", None, None, SPACE, None),
        P(SPACE, None),
        P(),
        P("tm"),
    )
    out_specs = (
        P("branch", "tm", None, SPACE, None),
        P("branch", "tm", None, SPACE, None),
        P("branch", None),
    )
    return jax.shard_map(
        on_device, mesh=finer, in_specs=in_specs, out_specs=out_specs, check_vma=False
    )
```

```python
import jax
import jax.numpy as jnp
from jax import lax
from jax.sharding import Mesh
from jax.sharding import PartitionSpec as P
from jax.experimental import pallas as pl

STEPS = 5
SPACE = ("space_0", "space_1")
TM_SPACE = ("tm", "space_0", "space_1")


TIME_STEP = 0.03
ACTIVATOR_DIFFUSION = 1.0
INHIBITOR_DIFFUSION = 6.0
REACTION_RATE = 2.5
SMALL_EPSILON = 1e-06
HIGHEST = lax.Precision.HIGHEST


def extended_2(cells, sides, width):
    for axis, dim in sides:
        count = lax.axis_size(axis)
        head = lax.slice_in_dim(cells, 0, width, axis=dim)
        tail = lax.slice_in_dim(cells, cells.shape[dim] - width, cells.shape[dim], axis=dim)
        cells = jnp.concatenate(
            [
                lax.ppermute(tail, axis, [(i, (i + 1) % count) for i in range(count)]),
                cells,
                lax.ppermute(head, axis, [((i + 1) % count, i) for i in range(count)]),
            ],
            axis=dim,
        )
    return cells


def swapped(value, axis, apart):
    mask = 2**apart
    pairs = [(source, source ^ mask) for source in range(lax.axis_size(axis))]
    return lax.ppermute(value, axis, pairs)


def passed_along(block, axis, distance):
    devices = range(lax.axis_size(axis))
    route = [((i - distance) % len(devices), i) for i in devices]
    return lax.ppermute(block, axis, route)


def butterfly_rounds(axes):
    rounds = []
    for axis in axes:
        count = lax.axis_size(axis)
        apart = 1
        while apart < count:
            rounds.append((axis, [(i, i ^ apart) for i in range(count)]))
            apart *= 2
    return rounds


def one_axis_at_a_time(x, axes):
    for axis, pairs in butterfly_rounds(axes):
        x = x + lax.ppermute(x, axis, pairs)
    return x


def laplacian_rows(extended):
    interior = extended[:, 1:-1, :]
    return (
        extended[:, 2:, :]
        + extended[:, :-2, :]
        + jnp.roll(interior, 1, 2)
        + jnp.roll(interior, -1, 2)
        - 4.0 * interior
    )


def advance(extended, feed_rate, active):
    laplacian = laplacian_rows(extended)
    interior = extended[:, 1:-1, :]
    activator = interior[0]
    inhibitor = interior[1]
    squared = activator * activator
    product = activator * inhibitor
    new_activator = activator + TIME_STEP * (
        ACTIVATOR_DIFFUSION * laplacian[0]
        + feed_rate
        - (REACTION_RATE + 1.0) * activator
        + squared * inhibitor
    )
    new_inhibitor = inhibitor + TIME_STEP * (
        INHIBITOR_DIFFUSION * laplacian[1] + REACTION_RATE * activator - squared * inhibitor
    )
    tangent_act = interior[2::2]
    tangent_inh = interior[3::2]
    new_tangent_act = tangent_act + TIME_STEP * (
        ACTIVATOR_DIFFUSION * laplacian[2::2]
        + (2.0 * product - REACTION_RATE - 1.0) * tangent_act
        + squared * tangent_inh
    )
    new_tangent_inh = tangent_inh + TIME_STEP * (
        INHIBITOR_DIFFUSION * laplacian[3::2]
        + (REACTION_RATE - 2.0 * product) * tangent_act
        - squared * tangent_inh
    )
    tangents = jnp.stack([new_tangent_act, new_tangent_inh], 1).reshape(
        tangent_act.shape[0] * 2, activator.shape[0], activator.shape[1]
    )
    advanced = jnp.concatenate([new_activator[None], new_inhibitor[None], tangents], 0)
    return jnp.where(active, advanced, interior)


def cholesky_kernel(gram_ref, rhs_ref, out_ref):
    size = gram_ref.shape[0]
    tile = gram_ref[...]
    rows = lax.broadcasted_iota(jnp.int32, tile.shape, 0)
    cols = lax.broadcasted_iota(jnp.int32, tile.shape, 1)
    diagonal = rows == cols
    index = rows[:, :1]
    columns = []
    pivots = []
    for outer in range(size):
        value = jnp.sum(jnp.where(cols == outer, tile, 0.0), axis=1, keepdims=True)
        pivot = jnp.sqrt(jnp.sum(jnp.where(index == outer, value, 0.0), axis=0, keepdims=True))
        column = jnp.where(index >= outer, value / pivot, 0.0)
        row = jnp.sum(jnp.where(diagonal, column, 0.0), axis=0, keepdims=True)
        tile = tile - column * row
        columns.append(column)
        pivots.append(pivot)
    accum = -jnp.sum(jnp.where(diagonal, rhs_ref[...], 0.0), axis=1, keepdims=True)
    middle = jnp.zeros_like(accum)
    for outer in range(size):
        value = jnp.sum(jnp.where(index == outer, accum, 0.0), axis=0, keepdims=True) / pivots[outer]
        middle = jnp.where(index == outer, value, middle)
        accum = accum - columns[outer] * value
    result = jnp.zeros_like(middle)
    for outer in range(size - 1, -1, -1):
        below = jnp.sum(jnp.where(index > outer, columns[outer] * result, 0.0), axis=0, keepdims=True)
        value = jnp.sum(jnp.where(index == outer, middle, 0.0), axis=0, keepdims=True)
        result = jnp.where(index == outer, (value - below) / pivots[outer], result)
    out_ref[...] = jnp.sum(jnp.where(diagonal, result, 0.0), axis=0, keepdims=True)


def solve_small(gram, rhs):
    size = gram.shape[0]
    lanes = 128
    padded = jnp.pad(gram, ((0, 0), (0, lanes - size)))
    rhs_row = jnp.pad(rhs, (0, lanes - size)).reshape(1, lanes)
    out = pl.pallas_call(
        cholesky_kernel, out_shape=jax.ShapeDtypeStruct((1, lanes), jnp.float32)
    )(padded, rhs_row)
    return out[0, :size]


def on_device(state, panel, region, feed_table, step_counts):
    start = state[0, 0]
    row_count = start.shape[1]
    column_count = start.shape[2]
    directions = panel.shape[2]
    tangent = panel[0, 0].reshape(2 * directions, row_count, column_count)
    stacked = jnp.concatenate([start, tangent], 0)
    following = passed_along(stacked, "tm", -1)
    partner_state = swapped(start, "branch", 0)
    classes = jnp.arange(feed_table.shape[0], dtype=jnp.int32)
    feed_rate = jnp.sum(
        jnp.where(region[None] == classes[:, None, None], feed_table[:, None, None], 0.0), 0
    )
    step_limit = step_counts[0]
    panel_rows = panel[0, 0].reshape(directions, -1)
    gap = (start - partner_state).reshape(-1)
    total = 2.0 * lax.axis_size("tm") * row_count * lax.axis_size(SPACE) * column_count
    gap_part = jnp.sum(gap * gap)
    along_part = jnp.dot(panel_rows, gap, precision=HIGHEST)
    first_sum = jnp.concatenate([gap_part[None], along_part])
    widened = extended_2(jnp.concatenate([stacked, feed_rate[None]], 0), ((SPACE, 1),), STEPS)
    stacked = widened[:-1]
    feed_wide = widened[-1]
    total_rows = feed_wide.shape[0]
    spread = {0: ("space_0",), 1: ("space_1",), 3: ("tm",)}
    for step_index in range(STEPS):
        stacked = advance(
            stacked,
            feed_wide[step_index + 1 : total_rows - step_index - 1],
            step_index < step_limit,
        )
        for axis, pairs in butterfly_rounds(spread.get(step_index, ())):
            first_sum = first_sum + lax.ppermute(first_sum, axis, pairs)
        stacked, first_sum = lax.optimization_barrier((stacked, first_sum))
    gap_sum = first_sum[0]
    along_sum = first_sum[1:]
    arrived = passed_along(stacked[:2], "tm", 1)
    mismatch = (arrived - start).reshape(-1)
    next_mismatch = (stacked[:2] - following[:2]).reshape(-1)
    next_jacobian = stacked[2:].reshape(directions, -1) - following[2:].reshape(directions, -1)
    distance = gap_sum / total + SMALL_EPSILON
    deflator = 1.0 / distance + 1.0
    slopes = -2.0 * (along_sum / total) / (distance * distance)
    deflated = deflator * mismatch
    next_deflated = deflator * next_mismatch
    deflated_panel = deflator * next_jacobian + slopes[:, None] * next_mismatch[None, :]
    gram_part = jnp.dot(deflated_panel, deflated_panel.T, precision=HIGHEST)
    rhs_part = jnp.dot(deflated_panel, next_deflated, precision=HIGHEST)
    second_sum = one_axis_at_a_time(
        jnp.concatenate([gram_part.reshape(-1), rhs_part]), TM_SPACE
    )
    gram = second_sum[: directions * directions].reshape(directions, directions) / total
    rhs = second_sum[directions * directions :] / total
    coefficients = solve_small(gram, rhs)
    correction = jnp.dot(coefficients, panel_rows, precision=HIGHEST)
    return (
        deflated.reshape(1, 1, 2, row_count, column_count),
        correction.reshape(1, 1, 2, row_count, column_count),
        coefficients.reshape(1, directions),
    )


def solution(mesh):
    finer = Mesh(
        mesh.devices.reshape(mesh.shape["tm"], 4, 4, mesh.shape["branch"]),
        ("tm", "space_0", "space_1", "branch"),
    )
    in_specs = (
        P("branch", "tm", None, SPACE, None),
        P("branch", "tm", None, None, SPACE, None),
        P(SPACE, None),
        P(),
        P("tm"),
    )
    out_specs = (
        P("branch", "tm", None, SPACE, None),
        P("branch", "tm", None, SPACE, None),
        P("branch", None),
    )
    return jax.shard_map(
        on_device, mesh=finer, in_specs=in_specs, out_specs=out_specs, check_vma=False
    )
```

```python
import jax
import jax.numpy as jnp
from jax import lax
from jax.sharding import Mesh
from jax.sharding import PartitionSpec as P
from jax.experimental import pallas as pl

STEPS = 5
SPACE = ("space_0", "space_1")
TM_SPACE = ("tm", "space_0", "space_1")


TIME_STEP = 0.03
ACTIVATOR_DIFFUSION = 1.0
INHIBITOR_DIFFUSION = 6.0
REACTION_RATE = 2.5
SMALL_EPSILON = 1e-06
HIGHEST = lax.Precision.HIGHEST


def extended_2(cells, sides, width):
    for axis, dim in sides:
        count = lax.axis_size(axis)
        head = lax.slice_in_dim(cells, 0, width, axis=dim)
        tail = lax.slice_in_dim(cells, cells.shape[dim] - width, cells.shape[dim], axis=dim)
        cells = jnp.concatenate(
            [
                lax.ppermute(tail, axis, [(i, (i + 1) % count) for i in range(count)]),
                cells,
                lax.ppermute(head, axis, [((i + 1) % count, i) for i in range(count)]),
            ],
            axis=dim,
        )
    return cells


def swapped(value, axis, apart):
    mask = 2**apart
    pairs = [(source, source ^ mask) for source in range(lax.axis_size(axis))]
    return lax.ppermute(value, axis, pairs)


def passed_along(block, axis, distance):
    devices = range(lax.axis_size(axis))
    route = [((i - distance) % len(devices), i) for i in devices]
    return lax.ppermute(block, axis, route)


def butterfly_rounds(axes):
    rounds = []
    for axis in axes:
        count = lax.axis_size(axis)
        apart = 1
        while apart < count:
            rounds.append((axis, [(i, i ^ apart) for i in range(count)]))
            apart *= 2
    return rounds


def one_axis_at_a_time(x, axes):
    for axis, pairs in butterfly_rounds(axes):
        x = x + lax.ppermute(x, axis, pairs)
    return x


def laplacian_rows(extended):
    interior = extended[..., 1:-1, :]
    return (
        extended[..., 2:, :]
        + extended[..., :-2, :]
        + jnp.roll(interior, 1, -1)
        + jnp.roll(interior, -1, -1)
        - 4.0 * interior
    )


def advance(fields, feed_rate, active):
    activator_wide, inhibitor_wide, tangent_act_wide, tangent_inh_wide = fields
    activator = activator_wide[1:-1]
    inhibitor = inhibitor_wide[1:-1]
    tangent_act = tangent_act_wide[:, 1:-1]
    tangent_inh = tangent_inh_wide[:, 1:-1]
    squared = activator * activator
    product = activator * inhibitor
    new_activator = activator + TIME_STEP * (
        ACTIVATOR_DIFFUSION * laplacian_rows(activator_wide)
        + feed_rate
        - (REACTION_RATE + 1.0) * activator
        + squared * inhibitor
    )
    new_inhibitor = inhibitor + TIME_STEP * (
        INHIBITOR_DIFFUSION * laplacian_rows(inhibitor_wide)
        + REACTION_RATE * activator
        - squared * inhibitor
    )
    new_tangent_act = tangent_act + TIME_STEP * (
        ACTIVATOR_DIFFUSION * laplacian_rows(tangent_act_wide)
        + (2.0 * product - REACTION_RATE - 1.0) * tangent_act
        + squared * tangent_inh
    )
    new_tangent_inh = tangent_inh + TIME_STEP * (
        INHIBITOR_DIFFUSION * laplacian_rows(tangent_inh_wide)
        + (REACTION_RATE - 2.0 * product) * tangent_act
        - squared * tangent_inh
    )
    return (
        jnp.where(active, new_activator, activator),
        jnp.where(active, new_inhibitor, inhibitor),
        jnp.where(active, new_tangent_act, tangent_act),
        jnp.where(active, new_tangent_inh, tangent_inh),
    )


def cholesky_kernel(gram_ref, rhs_ref, out_ref):
    size = gram_ref.shape[0]
    tile = gram_ref[...]
    rows = lax.broadcasted_iota(jnp.int32, tile.shape, 0)
    cols = lax.broadcasted_iota(jnp.int32, tile.shape, 1)
    diagonal = rows == cols
    index = rows[:, :1]
    columns = []
    pivots = []
    for outer in range(size):
        value = jnp.sum(jnp.where(cols == outer, tile, 0.0), axis=1, keepdims=True)
        pivot = jnp.sqrt(jnp.sum(jnp.where(index == outer, value, 0.0), axis=0, keepdims=True))
        column = jnp.where(index >= outer, value / pivot, 0.0)
        row = jnp.sum(jnp.where(diagonal, column, 0.0), axis=0, keepdims=True)
        tile = tile - column * row
        columns.append(column)
        pivots.append(pivot)
    accum = -jnp.sum(jnp.where(diagonal, rhs_ref[...], 0.0), axis=1, keepdims=True)
    middle = jnp.zeros_like(accum)
    for outer in range(size):
        value = jnp.sum(jnp.where(index == outer, accum, 0.0), axis=0, keepdims=True) / pivots[outer]
        middle = jnp.where(index == outer, value, middle)
        accum = accum - columns[outer] * value
    result = jnp.zeros_like(middle)
    for outer in range(size - 1, -1, -1):
        below = jnp.sum(jnp.where(index > outer, columns[outer] * result, 0.0), axis=0, keepdims=True)
        value = jnp.sum(jnp.where(index == outer, middle, 0.0), axis=0, keepdims=True)
        result = jnp.where(index == outer, (value - below) / pivots[outer], result)
    out_ref[...] = jnp.sum(jnp.where(diagonal, result, 0.0), axis=0, keepdims=True)


def solve_small(gram, rhs):
    size = gram.shape[0]
    lanes = 128
    padded = jnp.pad(gram, ((0, 0), (0, lanes - size)))
    rhs_row = jnp.pad(rhs, (0, lanes - size)).reshape(1, lanes)
    out = pl.pallas_call(
        cholesky_kernel, out_shape=jax.ShapeDtypeStruct((1, lanes), jnp.float32)
    )(padded, rhs_row)
    return out[0, :size]


def on_device(state, panel, region, feed_table, step_counts):
    start = state[0, 0]
    row_count = start.shape[1]
    column_count = start.shape[2]
    directions = panel.shape[2]
    tangent = panel[0, 0].reshape(2 * directions, row_count, column_count)
    stacked = jnp.concatenate([start, tangent], 0)
    following = passed_along(stacked, "tm", -1)
    partner_state = swapped(start, "branch", 0)
    classes = jnp.arange(feed_table.shape[0], dtype=jnp.int32)
    feed_rate = jnp.sum(
        jnp.where(region[None] == classes[:, None, None], feed_table[:, None, None], 0.0), 0
    )
    step_limit = step_counts[0]
    panel_rows = panel[0, 0].reshape(directions, -1)
    gap = (start - partner_state).reshape(-1)
    total = 2.0 * lax.axis_size("tm") * row_count * lax.axis_size(SPACE) * column_count
    gap_part = jnp.sum(gap * gap)
    along_part = jnp.dot(panel_rows, gap, precision=HIGHEST)
    first_sum = jnp.concatenate([gap_part[None], along_part])
    widened = extended_2(jnp.concatenate([stacked, feed_rate[None]], 0), ((SPACE, 1),), STEPS)
    fields = (widened[0], widened[1], widened[2:-1:2], widened[3:-1:2])
    feed_wide = widened[-1]
    total_rows = feed_wide.shape[0]
    spread = {0: ("space_0",), 1: ("space_1",), 3: ("tm",)}
    for step_index in range(STEPS):
        fields = advance(
            fields,
            feed_wide[step_index + 1 : total_rows - step_index - 1],
            step_index < step_limit,
        )
        for axis, pairs in butterfly_rounds(spread.get(step_index, ())):
            first_sum = first_sum + lax.ppermute(first_sum, axis, pairs)
        fields, first_sum = lax.optimization_barrier((fields, first_sum))
    end_state = jnp.stack(fields[:2], 0)
    end_tangent = jnp.stack(fields[2:], 1).reshape(directions, -1)
    gap_sum = first_sum[0]
    along_sum = first_sum[1:]
    arrived = passed_along(end_state, "tm", 1)
    mismatch = (arrived - start).reshape(-1)
    next_mismatch = (end_state - following[:2]).reshape(-1)
    next_jacobian = end_tangent - following[2:].reshape(directions, -1)
    distance = gap_sum / total + SMALL_EPSILON
    deflator = 1.0 / distance + 1.0
    slopes = -2.0 * (along_sum / total) / (distance * distance)
    deflated = deflator * mismatch
    next_deflated = deflator * next_mismatch
    deflated_panel = deflator * next_jacobian + slopes[:, None] * next_mismatch[None, :]
    gram_part = jnp.dot(deflated_panel, deflated_panel.T, precision=HIGHEST)
    rhs_part = jnp.dot(deflated_panel, next_deflated, precision=HIGHEST)
    deflated, second_sum = lax.optimization_barrier(
        (deflated, jnp.concatenate([gram_part.reshape(-1), rhs_part]))
    )
    second_sum = one_axis_at_a_time(second_sum, TM_SPACE)
    gram = second_sum[: directions * directions].reshape(directions, directions) / total
    rhs = second_sum[directions * directions :] / total
    coefficients = solve_small(gram, rhs)
    correction = jnp.dot(coefficients, panel_rows, precision=HIGHEST)
    return (
        deflated.reshape(1, 1, 2, row_count, column_count),
        correction.reshape(1, 1, 2, row_count, column_count),
        coefficients.reshape(1, directions),
    )


def solution(mesh):
    finer = Mesh(
        mesh.devices.reshape(mesh.shape["tm"], 4, 4, mesh.shape["branch"]),
        ("tm", "space_0", "space_1", "branch"),
    )
    in_specs = (
        P("branch", "tm", None, SPACE, None),
        P("branch", "tm", None, None, SPACE, None),
        P(SPACE, None),
        P(),
        P("tm"),
    )
    out_specs = (
        P("branch", "tm", None, SPACE, None),
        P("branch", "tm", None, SPACE, None),
        P("branch", None),
    )
    return jax.shard_map(
        on_device, mesh=finer, in_specs=in_specs, out_specs=out_specs, check_vma=False
    )
```

```python
import jax
import jax.numpy as jnp
from jax import lax
from jax.sharding import Mesh
from jax.sharding import PartitionSpec as P
from jax.experimental import pallas as pl

STEPS = 5
SPACE = ("space_0", "space_1")
TM_SPACE = ("tm", "space_0", "space_1")


TIME_STEP = 0.03
ACTIVATOR_DIFFUSION = 1.0
INHIBITOR_DIFFUSION = 6.0
REACTION_RATE = 2.5
SMALL_EPSILON = 1e-06
HIGHEST = lax.Precision.HIGHEST


def extended_2(cells, sides, width):
    for axis, dim in sides:
        count = lax.axis_size(axis)
        head = lax.slice_in_dim(cells, 0, width, axis=dim)
        tail = lax.slice_in_dim(cells, cells.shape[dim] - width, cells.shape[dim], axis=dim)
        cells = jnp.concatenate(
            [
                lax.ppermute(tail, axis, [(i, (i + 1) % count) for i in range(count)]),
                cells,
                lax.ppermute(head, axis, [((i + 1) % count, i) for i in range(count)]),
            ],
            axis=dim,
        )
    return cells


def swapped(value, axis, apart):
    mask = 2**apart
    pairs = [(source, source ^ mask) for source in range(lax.axis_size(axis))]
    return lax.ppermute(value, axis, pairs)


def passed_along(block, axis, distance):
    devices = range(lax.axis_size(axis))
    route = [((i - distance) % len(devices), i) for i in devices]
    return lax.ppermute(block, axis, route)


def butterfly_rounds(axes):
    rounds = []
    for axis in axes:
        count = lax.axis_size(axis)
        apart = 1
        while apart < count:
            rounds.append((axis, [(i, i ^ apart) for i in range(count)]))
            apart *= 2
    return rounds


def one_axis_at_a_time(x, axes):
    for axis, pairs in butterfly_rounds(axes):
        x = x + lax.ppermute(x, axis, pairs)
    return x


def laplacian_rows(extended):
    interior = extended[..., 1:-1, :]
    return (
        extended[..., 2:, :]
        + extended[..., :-2, :]
        + jnp.roll(interior, 1, -1)
        + jnp.roll(interior, -1, -1)
        - 4.0 * interior
    )


def advance(fields, feed_rate, active):
    activator_wide, inhibitor_wide, tangent_act_wide, tangent_inh_wide = fields
    activator = activator_wide[1:-1]
    inhibitor = inhibitor_wide[1:-1]
    tangent_act = tangent_act_wide[:, 1:-1]
    tangent_inh = tangent_inh_wide[:, 1:-1]
    squared = activator * activator
    product = activator * inhibitor
    new_activator = activator + TIME_STEP * (
        ACTIVATOR_DIFFUSION * laplacian_rows(activator_wide)
        + feed_rate
        - (REACTION_RATE + 1.0) * activator
        + squared * inhibitor
    )
    new_inhibitor = inhibitor + TIME_STEP * (
        INHIBITOR_DIFFUSION * laplacian_rows(inhibitor_wide)
        + REACTION_RATE * activator
        - squared * inhibitor
    )
    new_tangent_act = tangent_act + TIME_STEP * (
        ACTIVATOR_DIFFUSION * laplacian_rows(tangent_act_wide)
        + (2.0 * product - REACTION_RATE - 1.0) * tangent_act
        + squared * tangent_inh
    )
    new_tangent_inh = tangent_inh + TIME_STEP * (
        INHIBITOR_DIFFUSION * laplacian_rows(tangent_inh_wide)
        + (REACTION_RATE - 2.0 * product) * tangent_act
        - squared * tangent_inh
    )
    return (
        jnp.where(active, new_activator, activator),
        jnp.where(active, new_inhibitor, inhibitor),
        jnp.where(active, new_tangent_act, tangent_act),
        jnp.where(active, new_tangent_inh, tangent_inh),
    )


def cholesky_kernel(gram_ref, rhs_ref, out_ref):
    size = gram_ref.shape[0]
    tile = gram_ref[...]
    rows = lax.broadcasted_iota(jnp.int32, tile.shape, 0)
    cols = lax.broadcasted_iota(jnp.int32, tile.shape, 1)
    diagonal = rows == cols
    index = rows[:, :1]
    columns = []
    pivots = []
    for outer in range(size):
        value = jnp.sum(jnp.where(cols == outer, tile, 0.0), axis=1, keepdims=True)
        pivot = jnp.sqrt(jnp.sum(jnp.where(index == outer, value, 0.0), axis=0, keepdims=True))
        column = jnp.where(index >= outer, value / pivot, 0.0)
        row = jnp.sum(jnp.where(diagonal, column, 0.0), axis=0, keepdims=True)
        tile = tile - column * row
        columns.append(column)
        pivots.append(pivot)
    accum = -jnp.sum(jnp.where(diagonal, rhs_ref[...], 0.0), axis=1, keepdims=True)
    middle = jnp.zeros_like(accum)
    for outer in range(size):
        value = jnp.sum(jnp.where(index == outer, accum, 0.0), axis=0, keepdims=True) / pivots[outer]
        middle = jnp.where(index == outer, value, middle)
        accum = accum - columns[outer] * value
    result = jnp.zeros_like(middle)
    for outer in range(size - 1, -1, -1):
        below = jnp.sum(jnp.where(index > outer, columns[outer] * result, 0.0), axis=0, keepdims=True)
        value = jnp.sum(jnp.where(index == outer, middle, 0.0), axis=0, keepdims=True)
        result = jnp.where(index == outer, (value - below) / pivots[outer], result)
    out_ref[...] = jnp.sum(jnp.where(diagonal, result, 0.0), axis=0, keepdims=True)


def solve_small(gram, rhs):
    size = gram.shape[0]
    lanes = 128
    padded = jnp.pad(gram, ((0, 0), (0, lanes - size)))
    rhs_row = jnp.pad(rhs, (0, lanes - size)).reshape(1, lanes)
    out = pl.pallas_call(
        cholesky_kernel, out_shape=jax.ShapeDtypeStruct((1, lanes), jnp.float32)
    )(padded, rhs_row)
    return out[0, :size]


def on_device(state, panel, region, feed_table, step_counts):
    start = state[0, 0]
    row_count = start.shape[1]
    column_count = start.shape[2]
    directions = panel.shape[2]
    tangent = panel[0, 0].reshape(2 * directions, row_count, column_count)
    stacked = jnp.concatenate([start, tangent], 0)
    following = passed_along(stacked, "tm", -1)
    partner_state = swapped(start, "branch", 0)
    classes = jnp.arange(feed_table.shape[0], dtype=jnp.int32)
    feed_rate = jnp.sum(
        jnp.where(region[None] == classes[:, None, None], feed_table[:, None, None], 0.0), 0
    )
    step_limit = step_counts[0]
    panel_rows = panel[0, 0].reshape(directions, -1)
    gap = (start - partner_state).reshape(-1)
    total = 2.0 * lax.axis_size("tm") * row_count * lax.axis_size(SPACE) * column_count
    gap_part = jnp.sum(gap * gap)
    along_part = jnp.dot(panel_rows, gap, precision=HIGHEST)
    first_sum = jnp.concatenate([gap_part[None], along_part])
    widened = extended_2(jnp.concatenate([stacked, feed_rate[None]], 0), ((SPACE, 1),), STEPS)
    fields = (widened[0], widened[1], widened[2:-1:2], widened[3:-1:2])
    feed_wide = widened[-1]
    total_rows = feed_wide.shape[0]
    for step_index in range(STEPS):
        fields = advance(
            fields,
            feed_wide[step_index + 1 : total_rows - step_index - 1],
            step_index < step_limit,
        )
    end_state = jnp.stack(fields[:2], 0)
    end_tangent = jnp.stack(fields[2:], 1).reshape(directions, -1)
    arrived = passed_along(end_state, "tm", 1)
    next_mismatch = (end_state - following[:2]).reshape(-1)
    next_jacobian = end_tangent - following[2:].reshape(directions, -1)
    jacobian_gram = jnp.dot(next_jacobian, next_jacobian.T, precision=HIGHEST)
    jacobian_mismatch = jnp.dot(next_jacobian, next_mismatch, precision=HIGHEST)
    mismatch_square = jnp.sum(next_mismatch * next_mismatch)
    moments = one_axis_at_a_time(
        jnp.concatenate(
            [first_sum, mismatch_square[None], jacobian_mismatch, jacobian_gram.reshape(-1)]
        ),
        TM_SPACE,
    )
    gap_sum = moments[0]
    along_sum = moments[1 : 1 + directions]
    mismatch_sum = moments[1 + directions]
    cross_sum = moments[2 + directions : 2 + 2 * directions]
    jacobian_sum = moments[2 + 2 * directions :].reshape(directions, directions)
    distance = gap_sum / total + SMALL_EPSILON
    deflator = 1.0 / distance + 1.0
    slopes = -2.0 * (along_sum / total) / (distance * distance)
    mixed = deflator * slopes[:, None] * cross_sum[None, :]
    gram = (
        deflator * deflator * jacobian_sum
        + mixed
        + mixed.T
        + slopes[:, None] * slopes[None, :] * mismatch_sum
    ) / total
    rhs = (deflator * deflator * cross_sum + deflator * slopes * mismatch_sum) / total
    mismatch = (arrived - start).reshape(-1)
    deflated = deflator * mismatch
    coefficients = solve_small(gram, rhs)
    correction = jnp.dot(coefficients, panel_rows, precision=HIGHEST)
    return (
        deflated.reshape(1, 1, 2, row_count, column_count),
        correction.reshape(1, 1, 2, row_count, column_count),
        coefficients.reshape(1, directions),
    )


def solution(mesh):
    finer = Mesh(
        mesh.devices.reshape(mesh.shape["tm"], 4, 4, mesh.shape["branch"]),
        ("tm", "space_0", "space_1", "branch"),
    )
    in_specs = (
        P("branch", "tm", None, SPACE, None),
        P("branch", "tm", None, None, SPACE, None),
        P(SPACE, None),
        P(),
        P("tm"),
    )
    out_specs = (
        P("branch", "tm", None, SPACE, None),
        P("branch", "tm", None, SPACE, None),
        P("branch", None),
    )
    return jax.shard_map(
        on_device, mesh=finer, in_specs=in_specs, out_specs=out_specs, check_vma=False
    )
```

```python
import jax
import jax.numpy as jnp
from jax import lax
from jax.sharding import Mesh
from jax.sharding import PartitionSpec as P
from jax.experimental import pallas as pl

STEPS = 5
SPACE = ("space_0", "space_1")
TM_SPACE = ("tm", "space_0", "space_1")


TIME_STEP = 0.03
ACTIVATOR_DIFFUSION = 1.0
INHIBITOR_DIFFUSION = 6.0
REACTION_RATE = 2.5
SMALL_EPSILON = 1e-06
HIGHEST = lax.Precision.HIGHEST
HIGH = lax.Precision.HIGH


def extended_2(cells, sides, width):
    for axis, dim in sides:
        count = lax.axis_size(axis)
        head = lax.slice_in_dim(cells, 0, width, axis=dim)
        tail = lax.slice_in_dim(cells, cells.shape[dim] - width, cells.shape[dim], axis=dim)
        cells = jnp.concatenate(
            [
                lax.ppermute(tail, axis, [(i, (i + 1) % count) for i in range(count)]),
                cells,
                lax.ppermute(head, axis, [((i + 1) % count, i) for i in range(count)]),
            ],
            axis=dim,
        )
    return cells


def swapped(value, axis, apart):
    mask = 2**apart
    pairs = [(source, source ^ mask) for source in range(lax.axis_size(axis))]
    return lax.ppermute(value, axis, pairs)


def passed_along(block, axis, distance):
    devices = range(lax.axis_size(axis))
    route = [((i - distance) % len(devices), i) for i in devices]
    return lax.ppermute(block, axis, route)


def butterfly_rounds(axes):
    rounds = []
    for axis in axes:
        count = lax.axis_size(axis)
        apart = 1
        while apart < count:
            rounds.append((axis, [(i, i ^ apart) for i in range(count)]))
            apart *= 2
    return rounds


def one_axis_at_a_time(x, axes):
    for axis, pairs in butterfly_rounds(axes):
        x = x + lax.ppermute(x, axis, pairs)
    return x


def laplacian_rows(extended):
    interior = extended[..., 1:-1, :]
    return (
        extended[..., 2:, :]
        + extended[..., :-2, :]
        + jnp.roll(interior, 1, -1)
        + jnp.roll(interior, -1, -1)
        - 4.0 * interior
    )


def advance(fields, feed_rate, active):
    activator_wide, inhibitor_wide, tangent_act_wide, tangent_inh_wide = fields
    activator = activator_wide[1:-1]
    inhibitor = inhibitor_wide[1:-1]
    tangent_act = tangent_act_wide[:, 1:-1]
    tangent_inh = tangent_inh_wide[:, 1:-1]
    squared = activator * activator
    product = activator * inhibitor
    new_activator = activator + TIME_STEP * (
        ACTIVATOR_DIFFUSION * laplacian_rows(activator_wide)
        + feed_rate
        - (REACTION_RATE + 1.0) * activator
        + squared * inhibitor
    )
    new_inhibitor = inhibitor + TIME_STEP * (
        INHIBITOR_DIFFUSION * laplacian_rows(inhibitor_wide)
        + REACTION_RATE * activator
        - squared * inhibitor
    )
    new_tangent_act = tangent_act + TIME_STEP * (
        ACTIVATOR_DIFFUSION * laplacian_rows(tangent_act_wide)
        + (2.0 * product - REACTION_RATE - 1.0) * tangent_act
        + squared * tangent_inh
    )
    new_tangent_inh = tangent_inh + TIME_STEP * (
        INHIBITOR_DIFFUSION * laplacian_rows(tangent_inh_wide)
        + (REACTION_RATE - 2.0 * product) * tangent_act
        - squared * tangent_inh
    )
    return (
        jnp.where(active, new_activator, activator),
        jnp.where(active, new_inhibitor, inhibitor),
        jnp.where(active, new_tangent_act, tangent_act),
        jnp.where(active, new_tangent_inh, tangent_inh),
    )


def cholesky_kernel(gram_ref, rhs_ref, out_ref):
    size = gram_ref.shape[0]
    tile = gram_ref[...]
    rows = lax.broadcasted_iota(jnp.int32, tile.shape, 0)
    cols = lax.broadcasted_iota(jnp.int32, tile.shape, 1)
    diagonal = rows == cols
    index = rows[:, :1]
    columns = []
    pivots = []
    for outer in range(size):
        value = jnp.sum(jnp.where(cols == outer, tile, 0.0), axis=1, keepdims=True)
        pivot = jnp.sqrt(jnp.sum(jnp.where(index == outer, value, 0.0), axis=0, keepdims=True))
        column = jnp.where(index >= outer, value / pivot, 0.0)
        row = jnp.sum(jnp.where(diagonal, column, 0.0), axis=0, keepdims=True)
        tile = tile - column * row
        columns.append(column)
        pivots.append(pivot)
    accum = -jnp.sum(jnp.where(diagonal, rhs_ref[...], 0.0), axis=1, keepdims=True)
    middle = jnp.zeros_like(accum)
    for outer in range(size):
        value = jnp.sum(jnp.where(index == outer, accum, 0.0), axis=0, keepdims=True) / pivots[outer]
        middle = jnp.where(index == outer, value, middle)
        accum = accum - columns[outer] * value
    result = jnp.zeros_like(middle)
    for outer in range(size - 1, -1, -1):
        below = jnp.sum(jnp.where(index > outer, columns[outer] * result, 0.0), axis=0, keepdims=True)
        value = jnp.sum(jnp.where(index == outer, middle, 0.0), axis=0, keepdims=True)
        result = jnp.where(index == outer, (value - below) / pivots[outer], result)
    out_ref[...] = jnp.sum(jnp.where(diagonal, result, 0.0), axis=0, keepdims=True)


def solve_small(gram, rhs):
    size = gram.shape[0]
    lanes = 128
    padded = jnp.pad(gram, ((0, 0), (0, lanes - size)))
    rhs_row = jnp.pad(rhs, (0, lanes - size)).reshape(1, lanes)
    out = pl.pallas_call(
        cholesky_kernel, out_shape=jax.ShapeDtypeStruct((1, lanes), jnp.float32)
    )(padded, rhs_row)
    return out[0, :size]


def on_device(state, panel, region, feed_table, step_counts):
    start = state[0, 0]
    row_count = start.shape[1]
    column_count = start.shape[2]
    directions = panel.shape[2]
    tangent = panel[0, 0].reshape(2 * directions, row_count, column_count)
    stacked = jnp.concatenate([start, tangent], 0)
    partner_state = swapped(start, "branch", 0)
    classes = jnp.arange(feed_table.shape[0], dtype=jnp.int32)
    feed_rate = jnp.sum(
        jnp.where(region[None] == classes[:, None, None], feed_table[:, None, None], 0.0), 0
    )
    step_limit = step_counts[0]
    panel_rows = panel[0, 0].reshape(directions, -1)
    gap = (start - partner_state).reshape(-1)
    total = 2.0 * lax.axis_size("tm") * row_count * lax.axis_size(SPACE) * column_count
    gap_part = jnp.sum(gap * gap)
    along_part = jnp.dot(panel_rows, gap, precision=HIGHEST)
    first_sum = jnp.concatenate([gap_part[None], along_part])
    widened = extended_2(jnp.concatenate([stacked, feed_rate[None]], 0), ((SPACE, 1),), STEPS)
    widened, sent = lax.optimization_barrier((widened, stacked))
    following = passed_along(sent, "tm", -1)
    fields = (widened[0], widened[1], widened[2:-1:2], widened[3:-1:2])
    feed_wide = widened[-1]
    total_rows = feed_wide.shape[0]
    for step_index in range(STEPS):
        fields = advance(
            fields,
            feed_wide[step_index + 1 : total_rows - step_index - 1],
            step_index < step_limit,
        )
    end_state = jnp.stack(fields[:2], 0)
    end_tangent = jnp.stack(fields[2:], 1).reshape(directions, -1)
    arrived = passed_along(end_state, "tm", 1)
    next_mismatch = (end_state - following[:2]).reshape(-1)
    next_jacobian = end_tangent - following[2:].reshape(directions, -1)
    jacobian_gram = jnp.dot(next_jacobian, next_jacobian.T, precision=HIGH)
    jacobian_mismatch = jnp.dot(next_jacobian, next_mismatch, precision=HIGH)
    mismatch_square = jnp.sum(next_mismatch * next_mismatch)
    moments = one_axis_at_a_time(
        jnp.concatenate(
            [first_sum, mismatch_square[None], jacobian_mismatch, jacobian_gram.reshape(-1)]
        ),
        TM_SPACE,
    )
    gap_sum = moments[0]
    along_sum = moments[1 : 1 + directions]
    mismatch_sum = moments[1 + directions]
    cross_sum = moments[2 + directions : 2 + 2 * directions]
    jacobian_sum = moments[2 + 2 * directions :].reshape(directions, directions)
    distance = gap_sum / total + SMALL_EPSILON
    deflator = 1.0 / distance + 1.0
    slopes = -2.0 * (along_sum / total) / (distance * distance)
    mixed = deflator * slopes[:, None] * cross_sum[None, :]
    gram = (
        deflator * deflator * jacobian_sum
        + mixed
        + mixed.T
        + slopes[:, None] * slopes[None, :] * mismatch_sum
    ) / total
    rhs = (deflator * deflator * cross_sum + deflator * slopes * mismatch_sum) / total
    mismatch = (arrived - start).reshape(-1)
    deflated = deflator * mismatch
    coefficients = solve_small(gram, rhs)
    correction = jnp.dot(coefficients, panel_rows, precision=HIGH)
    return (
        deflated.reshape(1, 1, 2, row_count, column_count),
        correction.reshape(1, 1, 2, row_count, column_count),
        coefficients.reshape(1, directions),
    )


def solution(mesh):
    finer = Mesh(
        mesh.devices.reshape(mesh.shape["tm"], 4, 4, mesh.shape["branch"]),
        ("tm", "space_0", "space_1", "branch"),
    )
    in_specs = (
        P("branch", "tm", None, SPACE, None),
        P("branch", "tm", None, None, SPACE, None),
        P(SPACE, None),
        P(),
        P("tm"),
    )
    out_specs = (
        P("branch", "tm", None, SPACE, None),
        P("branch", "tm", None, SPACE, None),
        P("branch", None),
    )
    return jax.shard_map(
        on_device, mesh=finer, in_specs=in_specs, out_specs=out_specs, check_vma=False
    )
```

```python
import jax
import jax.numpy as jnp
from jax import lax
from jax.sharding import Mesh
from jax.sharding import PartitionSpec as P
from jax.experimental import pallas as pl

STEPS = 5
SPACE = ("space_0", "space_1")
TM_SPACE = ("tm", "space_0", "space_1")


TIME_STEP = 0.03
ACTIVATOR_DIFFUSION = 1.0
INHIBITOR_DIFFUSION = 6.0
REACTION_RATE = 2.5
SMALL_EPSILON = 1e-06
HIGHEST = lax.Precision.HIGHEST
HIGH = lax.Precision.HIGH


def split_permute(block, axis, pairs):
    cut = block.shape[0] // 2
    return jnp.concatenate(
        [lax.ppermute(block[:cut], axis, pairs), lax.ppermute(block[cut:], axis, pairs)], 0
    )


def extended_2(cells, sides, width):
    for axis, dim in sides:
        count = lax.axis_size(axis)
        head = lax.slice_in_dim(cells, 0, width, axis=dim)
        tail = lax.slice_in_dim(cells, cells.shape[dim] - width, cells.shape[dim], axis=dim)
        cells = jnp.concatenate(
            [
                split_permute(tail, axis, [(i, (i + 1) % count) for i in range(count)]),
                cells,
                split_permute(head, axis, [((i + 1) % count, i) for i in range(count)]),
            ],
            axis=dim,
        )
    return cells


def swapped(value, axis, apart):
    mask = 2**apart
    pairs = [(source, source ^ mask) for source in range(lax.axis_size(axis))]
    return lax.ppermute(value, axis, pairs)


def passed_along(block, axis, distance):
    devices = range(lax.axis_size(axis))
    route = [((i - distance) % len(devices), i) for i in devices]
    return lax.ppermute(block, axis, route)


def butterfly_rounds(axes):
    rounds = []
    for axis in axes:
        count = lax.axis_size(axis)
        apart = 1
        while apart < count:
            rounds.append((axis, [(i, i ^ apart) for i in range(count)]))
            apart *= 2
    return rounds


def one_axis_at_a_time(x, axes):
    for axis, pairs in butterfly_rounds(axes):
        x = x + lax.ppermute(x, axis, pairs)
    return x


def laplacian_rows(extended):
    interior = extended[..., 1:-1, :]
    return (
        extended[..., 2:, :]
        + extended[..., :-2, :]
        + jnp.roll(interior, 1, -1)
        + jnp.roll(interior, -1, -1)
        - 4.0 * interior
    )


def advance(fields, feed_rate, active):
    activator_wide, inhibitor_wide, tangent_act_wide, tangent_inh_wide = fields
    activator = activator_wide[1:-1]
    inhibitor = inhibitor_wide[1:-1]
    tangent_act = tangent_act_wide[:, 1:-1]
    tangent_inh = tangent_inh_wide[:, 1:-1]
    squared = activator * activator
    product = activator * inhibitor
    new_activator = activator + TIME_STEP * (
        ACTIVATOR_DIFFUSION * laplacian_rows(activator_wide)
        + feed_rate
        - (REACTION_RATE + 1.0) * activator
        + squared * inhibitor
    )
    new_inhibitor = inhibitor + TIME_STEP * (
        INHIBITOR_DIFFUSION * laplacian_rows(inhibitor_wide)
        + REACTION_RATE * activator
        - squared * inhibitor
    )
    new_tangent_act = tangent_act + TIME_STEP * (
        ACTIVATOR_DIFFUSION * laplacian_rows(tangent_act_wide)
        + (2.0 * product - REACTION_RATE - 1.0) * tangent_act
        + squared * tangent_inh
    )
    new_tangent_inh = tangent_inh + TIME_STEP * (
        INHIBITOR_DIFFUSION * laplacian_rows(tangent_inh_wide)
        + (REACTION_RATE - 2.0 * product) * tangent_act
        - squared * tangent_inh
    )
    return (
        jnp.where(active, new_activator, activator),
        jnp.where(active, new_inhibitor, inhibitor),
        jnp.where(active, new_tangent_act, tangent_act),
        jnp.where(active, new_tangent_inh, tangent_inh),
    )


def cholesky_kernel(gram_ref, rhs_ref, out_ref):
    size = gram_ref.shape[0]
    tile = gram_ref[...]
    rows = lax.broadcasted_iota(jnp.int32, tile.shape, 0)
    cols = lax.broadcasted_iota(jnp.int32, tile.shape, 1)
    diagonal = rows == cols
    index = rows[:, :1]
    columns = []
    pivots = []
    for outer in range(size):
        value = jnp.sum(jnp.where(cols == outer, tile, 0.0), axis=1, keepdims=True)
        pivot = jnp.sqrt(jnp.sum(jnp.where(index == outer, value, 0.0), axis=0, keepdims=True))
        column = jnp.where(index >= outer, value / pivot, 0.0)
        row = jnp.sum(jnp.where(diagonal, column, 0.0), axis=0, keepdims=True)
        tile = tile - column * row
        columns.append(column)
        pivots.append(pivot)
    accum = -jnp.sum(jnp.where(diagonal, rhs_ref[...], 0.0), axis=1, keepdims=True)
    middle = jnp.zeros_like(accum)
    for outer in range(size):
        value = jnp.sum(jnp.where(index == outer, accum, 0.0), axis=0, keepdims=True) / pivots[outer]
        middle = jnp.where(index == outer, value, middle)
        accum = accum - columns[outer] * value
    result = jnp.zeros_like(middle)
    for outer in range(size - 1, -1, -1):
        below = jnp.sum(jnp.where(index > outer, columns[outer] * result, 0.0), axis=0, keepdims=True)
        value = jnp.sum(jnp.where(index == outer, middle, 0.0), axis=0, keepdims=True)
        result = jnp.where(index == outer, (value - below) / pivots[outer], result)
    out_ref[...] = jnp.sum(jnp.where(diagonal, result, 0.0), axis=0, keepdims=True)


def solve_small(gram, rhs):
    size = gram.shape[0]
    lanes = 128
    padded = jnp.pad(gram, ((0, 0), (0, lanes - size)))
    rhs_row = jnp.pad(rhs, (0, lanes - size)).reshape(1, lanes)
    out = pl.pallas_call(
        cholesky_kernel, out_shape=jax.ShapeDtypeStruct((1, lanes), jnp.float32)
    )(padded, rhs_row)
    return out[0, :size]


def on_device(state, panel, region, feed_table, step_counts):
    start = state[0, 0]
    row_count = start.shape[1]
    column_count = start.shape[2]
    directions = panel.shape[2]
    tangent = panel[0, 0].reshape(2 * directions, row_count, column_count)
    stacked = jnp.concatenate([start, tangent], 0)
    following = jnp.concatenate(
        [passed_along(part, "tm", -1) for part in jnp.split(stacked, [stacked.shape[0] // 2])], 0
    )
    partner_state = swapped(start, "branch", 0)
    classes = jnp.arange(feed_table.shape[0], dtype=jnp.int32)
    feed_rate = jnp.sum(
        jnp.where(region[None] == classes[:, None, None], feed_table[:, None, None], 0.0), 0
    )
    step_limit = step_counts[0]
    panel_rows = panel[0, 0].reshape(directions, -1)
    gap = (start - partner_state).reshape(-1)
    total = 2.0 * lax.axis_size("tm") * row_count * lax.axis_size(SPACE) * column_count
    gap_part = jnp.sum(gap * gap)
    along_part = jnp.dot(panel_rows, gap, precision=HIGHEST)
    first_sum = jnp.concatenate([gap_part[None], along_part])
    widened = extended_2(jnp.concatenate([stacked, feed_rate[None]], 0), ((SPACE, 1),), STEPS)
    fields = (widened[0], widened[1], widened[2:-1:2], widened[3:-1:2])
    feed_wide = widened[-1]
    total_rows = feed_wide.shape[0]
    for step_index in range(STEPS):
        fields = advance(
            fields,
            feed_wide[step_index + 1 : total_rows - step_index - 1],
            step_index < step_limit,
        )
    end_state = jnp.stack(fields[:2], 0)
    end_tangent = jnp.stack(fields[2:], 1).reshape(directions, -1)
    arrived = passed_along(end_state, "tm", 1)
    next_mismatch = (end_state - following[:2]).reshape(-1)
    next_jacobian = end_tangent - following[2:].reshape(directions, -1)
    jacobian_gram = jnp.dot(next_jacobian, next_jacobian.T, precision=HIGH)
    jacobian_mismatch = jnp.dot(next_jacobian, next_mismatch, precision=HIGH)
    mismatch_square = jnp.sum(next_mismatch * next_mismatch)
    moments = one_axis_at_a_time(
        jnp.concatenate(
            [first_sum, mismatch_square[None], jacobian_mismatch, jacobian_gram.reshape(-1)]
        ),
        TM_SPACE,
    )
    gap_sum = moments[0]
    along_sum = moments[1 : 1 + directions]
    mismatch_sum = moments[1 + directions]
    cross_sum = moments[2 + directions : 2 + 2 * directions]
    jacobian_sum = moments[2 + 2 * directions :].reshape(directions, directions)
    distance = gap_sum / total + SMALL_EPSILON
    deflator = 1.0 / distance + 1.0
    slopes = -2.0 * (along_sum / total) / (distance * distance)
    mixed = deflator * slopes[:, None] * cross_sum[None, :]
    gram = (
        deflator * deflator * jacobian_sum
        + mixed
        + mixed.T
        + slopes[:, None] * slopes[None, :] * mismatch_sum
    ) / total
    rhs = (deflator * deflator * cross_sum + deflator * slopes * mismatch_sum) / total
    mismatch = (arrived - start).reshape(-1)
    deflated = deflator * mismatch
    coefficients = solve_small(gram, rhs)
    correction = jnp.dot(coefficients, panel_rows, precision=HIGH)
    return (
        deflated.reshape(1, 1, 2, row_count, column_count),
        correction.reshape(1, 1, 2, row_count, column_count),
        coefficients.reshape(1, directions),
    )


def solution(mesh):
    finer = Mesh(
        mesh.devices.reshape(mesh.shape["tm"], 4, 4, mesh.shape["branch"]),
        ("tm", "space_0", "space_1", "branch"),
    )
    in_specs = (
        P("branch", "tm", None, SPACE, None),
        P("branch", "tm", None, None, SPACE, None),
        P(SPACE, None),
        P(),
        P("tm"),
    )
    out_specs = (
        P("branch", "tm", None, SPACE, None),
        P("branch", "tm", None, SPACE, None),
        P("branch", None),
    )
    return jax.shard_map(
        on_device, mesh=finer, in_specs=in_specs, out_specs=out_specs, check_vma=False
    )
```

```python
import jax
import jax.numpy as jnp
from jax import lax
from jax.sharding import Mesh
from jax.sharding import PartitionSpec as P
from jax.experimental import pallas as pl

STEPS = 5
SPACE = ("space_0", "space_1")
TM_SPACE = ("tm", "space_0", "space_1")


TIME_STEP = 0.03
ACTIVATOR_DIFFUSION = 1.0
INHIBITOR_DIFFUSION = 6.0
REACTION_RATE = 2.5
SMALL_EPSILON = 1e-06
HIGHEST = lax.Precision.HIGHEST
HIGH = lax.Precision.HIGH


def extended_2(cells, sides, width):
    for axis, dim in sides:
        count = lax.axis_size(axis)
        head = lax.slice_in_dim(cells, 0, width, axis=dim)
        tail = lax.slice_in_dim(cells, cells.shape[dim] - width, cells.shape[dim], axis=dim)
        cells = jnp.concatenate(
            [
                lax.ppermute(tail, axis, [(i, (i + 1) % count) for i in range(count)]),
                cells,
                lax.ppermute(head, axis, [((i + 1) % count, i) for i in range(count)]),
            ],
            axis=dim,
        )
    return cells


def swapped(value, axis, apart):
    mask = 2**apart
    pairs = [(source, source ^ mask) for source in range(lax.axis_size(axis))]
    return lax.ppermute(value, axis, pairs)


def passed_along(block, axis, distance):
    devices = range(lax.axis_size(axis))
    route = [((i - distance) % len(devices), i) for i in devices]
    return lax.ppermute(block, axis, route)


def butterfly_rounds(axes):
    rounds = []
    for axis in axes:
        count = lax.axis_size(axis)
        apart = 1
        while apart < count:
            rounds.append((axis, [(i, i ^ apart) for i in range(count)]))
            apart *= 2
    return rounds


def one_axis_at_a_time(x, axes):
    for axis, pairs in butterfly_rounds(axes):
        x = x + lax.ppermute(x, axis, pairs)
    return x


def laplacian_rows(extended):
    interior = extended[..., 1:-1, :]
    return (
        extended[..., 2:, :]
        + extended[..., :-2, :]
        + jnp.roll(interior, 1, -1)
        + jnp.roll(interior, -1, -1)
        - 4.0 * interior
    )


def advance(fields, feed_rate, active):
    activator_wide, inhibitor_wide, tangent_act_wide, tangent_inh_wide = fields
    activator = activator_wide[1:-1]
    inhibitor = inhibitor_wide[1:-1]
    tangent_act = tangent_act_wide[:, 1:-1]
    tangent_inh = tangent_inh_wide[:, 1:-1]
    squared = activator * activator
    product = activator * inhibitor
    new_activator = activator + TIME_STEP * (
        ACTIVATOR_DIFFUSION * laplacian_rows(activator_wide)
        + feed_rate
        - (REACTION_RATE + 1.0) * activator
        + squared * inhibitor
    )
    new_inhibitor = inhibitor + TIME_STEP * (
        INHIBITOR_DIFFUSION * laplacian_rows(inhibitor_wide)
        + REACTION_RATE * activator
        - squared * inhibitor
    )
    new_tangent_act = tangent_act + TIME_STEP * (
        ACTIVATOR_DIFFUSION * laplacian_rows(tangent_act_wide)
        + (2.0 * product - REACTION_RATE - 1.0) * tangent_act
        + squared * tangent_inh
    )
    new_tangent_inh = tangent_inh + TIME_STEP * (
        INHIBITOR_DIFFUSION * laplacian_rows(tangent_inh_wide)
        + (REACTION_RATE - 2.0 * product) * tangent_act
        - squared * tangent_inh
    )
    return (
        jnp.where(active, new_activator, activator),
        jnp.where(active, new_inhibitor, inhibitor),
        jnp.where(active, new_tangent_act, tangent_act),
        jnp.where(active, new_tangent_inh, tangent_inh),
    )


def cholesky_kernel(gram_ref, rhs_ref, out_ref):
    size = gram_ref.shape[0]
    tile = gram_ref[...]
    rows = lax.broadcasted_iota(jnp.int32, tile.shape, 0)
    cols = lax.broadcasted_iota(jnp.int32, tile.shape, 1)
    diagonal = rows == cols
    index = rows[:, :1]
    columns = []
    pivots = []
    for outer in range(size):
        value = jnp.sum(jnp.where(cols == outer, tile, 0.0), axis=1, keepdims=True)
        pivot = jnp.sqrt(jnp.sum(jnp.where(index == outer, value, 0.0), axis=0, keepdims=True))
        column = jnp.where(index >= outer, value / pivot, 0.0)
        row = jnp.sum(jnp.where(diagonal, column, 0.0), axis=0, keepdims=True)
        tile = tile - column * row
        columns.append(column)
        pivots.append(pivot)
    accum = -jnp.sum(jnp.where(diagonal, rhs_ref[...], 0.0), axis=1, keepdims=True)
    middle = jnp.zeros_like(accum)
    for outer in range(size):
        value = jnp.sum(jnp.where(index == outer, accum, 0.0), axis=0, keepdims=True) / pivots[outer]
        middle = jnp.where(index == outer, value, middle)
        accum = accum - columns[outer] * value
    result = jnp.zeros_like(middle)
    for outer in range(size - 1, -1, -1):
        below = jnp.sum(jnp.where(index > outer, columns[outer] * result, 0.0), axis=0, keepdims=True)
        value = jnp.sum(jnp.where(index == outer, middle, 0.0), axis=0, keepdims=True)
        result = jnp.where(index == outer, (value - below) / pivots[outer], result)
    out_ref[...] = jnp.sum(jnp.where(diagonal, result, 0.0), axis=0, keepdims=True)


def solve_small(gram, rhs):
    size = gram.shape[0]
    lanes = 128
    padded = jnp.pad(gram, ((0, 0), (0, lanes - size)))
    rhs_row = jnp.pad(rhs, (0, lanes - size)).reshape(1, lanes)
    out = pl.pallas_call(
        cholesky_kernel, out_shape=jax.ShapeDtypeStruct((1, lanes), jnp.float32)
    )(padded, rhs_row)
    return out[0, :size]


def on_device(state, panel, region, feed_table, step_counts):
    start = state[0, 0]
    row_count = start.shape[1]
    column_count = start.shape[2]
    directions = panel.shape[2]
    tangent = panel[0, 0].reshape(2 * directions, row_count, column_count)
    stacked = jnp.concatenate([start, tangent], 0)
    following = passed_along(stacked, "tm", -1)
    partner_state = swapped(start, "branch", 0)
    classes = jnp.arange(feed_table.shape[0], dtype=jnp.int32)
    feed_rate = jnp.sum(
        jnp.where(region[None] == classes[:, None, None], feed_table[:, None, None], 0.0), 0
    )
    step_limit = step_counts[0]
    panel_rows = panel[0, 0].reshape(directions, -1)
    gap = (start - partner_state).reshape(-1)
    total = 2.0 * lax.axis_size("tm") * row_count * lax.axis_size(SPACE) * column_count
    gap_part = jnp.sum(gap * gap)
    along_part = jnp.dot(panel_rows, gap, precision=HIGHEST)
    first_sum = jnp.concatenate([gap_part[None], along_part])
    widened = extended_2(jnp.concatenate([stacked, feed_rate[None]], 0), ((SPACE, 1),), STEPS)
    fields = (widened[0], widened[1], widened[2:-1:2], widened[3:-1:2])
    feed_wide = widened[-1]
    total_rows = feed_wide.shape[0]
    for step_index in range(STEPS):
        fields = advance(
            fields,
            feed_wide[step_index + 1 : total_rows - step_index - 1],
            step_index < step_limit,
        )
    end_state = jnp.stack(fields[:2], 0)
    end_tangent = jnp.stack(fields[2:], 1).reshape(directions, -1)
    arrived = passed_along(end_state, "tm", 1)
    next_mismatch = (end_state - following[:2]).reshape(-1)
    next_jacobian = end_tangent - following[2:].reshape(directions, -1)
    jacobian_gram = jnp.dot(next_jacobian, next_jacobian.T, precision=HIGH)
    jacobian_mismatch = jnp.dot(next_jacobian, next_mismatch, precision=HIGH)
    mismatch_square = jnp.sum(next_mismatch * next_mismatch)
    moments = one_axis_at_a_time(
        jnp.concatenate(
            [first_sum, mismatch_square[None], jacobian_mismatch, jacobian_gram.reshape(-1)]
        ),
        TM_SPACE,
    )
    gap_sum = moments[0]
    along_sum = moments[1 : 1 + directions]
    mismatch_sum = moments[1 + directions]
    cross_sum = moments[2 + directions : 2 + 2 * directions]
    jacobian_sum = moments[2 + 2 * directions :].reshape(directions, directions)
    distance = gap_sum / total + SMALL_EPSILON
    deflator = 1.0 / distance + 1.0
    slopes = -2.0 * (along_sum / total) / (distance * distance)
    mixed = deflator * slopes[:, None] * cross_sum[None, :]
    gram = (
        deflator * deflator * jacobian_sum
        + mixed
        + mixed.T
        + slopes[:, None] * slopes[None, :] * mismatch_sum
    ) / total
    rhs = (deflator * deflator * cross_sum + deflator * slopes * mismatch_sum) / total
    mismatch = (arrived - start).reshape(-1)
    deflated = deflator * mismatch
    coefficients = solve_small(gram, rhs)
    correction = jnp.sum(coefficients[:, None, None, None] * panel[0, 0], 0)
    return (
        deflated.reshape(1, 1, 2, row_count, column_count),
        correction.reshape(1, 1, 2, row_count, column_count),
        coefficients.reshape(1, directions),
    )


def solution(mesh):
    finer = Mesh(
        mesh.devices.reshape(mesh.shape["tm"], 4, 4, mesh.shape["branch"]),
        ("tm", "space_0", "space_1", "branch"),
    )
    in_specs = (
        P("branch", "tm", None, SPACE, None),
        P("branch", "tm", None, None, SPACE, None),
        P(SPACE, None),
        P(),
        P("tm"),
    )
    out_specs = (
        P("branch", "tm", None, SPACE, None),
        P("branch", "tm", None, SPACE, None),
        P("branch", None),
    )
    return jax.shard_map(
        on_device, mesh=finer, in_specs=in_specs, out_specs=out_specs, check_vma=False
    )
```

```python
import functools

import jax
import jax.numpy as jnp
from jax import lax
from jax.sharding import Mesh
from jax.sharding import PartitionSpec as P
from jax.experimental import pallas as pl

STEPS = 5
SPACE = ("space_0", "space_1")
TM_SPACE = ("tm", "space_0", "space_1")


TIME_STEP = 0.03
ACTIVATOR_DIFFUSION = 1.0
INHIBITOR_DIFFUSION = 6.0
REACTION_RATE = 2.5
SMALL_EPSILON = 1e-06
HIGHEST = lax.Precision.HIGHEST
HIGH = lax.Precision.HIGH


def extended_2(cells, sides, width):
    for axis, dim in sides:
        count = lax.axis_size(axis)
        head = lax.slice_in_dim(cells, 0, width, axis=dim)
        tail = lax.slice_in_dim(cells, cells.shape[dim] - width, cells.shape[dim], axis=dim)
        cells = jnp.concatenate(
            [
                lax.ppermute(tail, axis, [(i, (i + 1) % count) for i in range(count)]),
                cells,
                lax.ppermute(head, axis, [((i + 1) % count, i) for i in range(count)]),
            ],
            axis=dim,
        )
    return cells


def swapped(value, axis, apart):
    mask = 2**apart
    pairs = [(source, source ^ mask) for source in range(lax.axis_size(axis))]
    return lax.ppermute(value, axis, pairs)


def passed_along(block, axis, distance):
    devices = range(lax.axis_size(axis))
    route = [((i - distance) % len(devices), i) for i in devices]
    return lax.ppermute(block, axis, route)


def butterfly_rounds(axes):
    rounds = []
    for axis in axes:
        count = lax.axis_size(axis)
        apart = 1
        while apart < count:
            rounds.append((axis, [(i, i ^ apart) for i in range(count)]))
            apart *= 2
    return rounds


def one_axis_at_a_time(x, axes):
    for axis, pairs in butterfly_rounds(axes):
        x = x + lax.ppermute(x, axis, pairs)
    return x


def laplacian_rows(extended):
    interior = extended[..., 1:-1, :]
    return (
        extended[..., 2:, :]
        + extended[..., :-2, :]
        + jnp.roll(interior, 1, -1)
        + jnp.roll(interior, -1, -1)
        - 4.0 * interior
    )


def advance(fields, feed_rate, active):
    activator_wide, inhibitor_wide, tangent_act_wide, tangent_inh_wide = fields
    activator = activator_wide[1:-1]
    inhibitor = inhibitor_wide[1:-1]
    tangent_act = tangent_act_wide[:, 1:-1]
    tangent_inh = tangent_inh_wide[:, 1:-1]
    squared = activator * activator
    product = activator * inhibitor
    new_activator = activator + TIME_STEP * (
        ACTIVATOR_DIFFUSION * laplacian_rows(activator_wide)
        + feed_rate
        - (REACTION_RATE + 1.0) * activator
        + squared * inhibitor
    )
    new_inhibitor = inhibitor + TIME_STEP * (
        INHIBITOR_DIFFUSION * laplacian_rows(inhibitor_wide)
        + REACTION_RATE * activator
        - squared * inhibitor
    )
    new_tangent_act = tangent_act + TIME_STEP * (
        ACTIVATOR_DIFFUSION * laplacian_rows(tangent_act_wide)
        + (2.0 * product - REACTION_RATE - 1.0) * tangent_act
        + squared * tangent_inh
    )
    new_tangent_inh = tangent_inh + TIME_STEP * (
        INHIBITOR_DIFFUSION * laplacian_rows(tangent_inh_wide)
        + (REACTION_RATE - 2.0 * product) * tangent_act
        - squared * tangent_inh
    )
    return (
        jnp.where(active, new_activator, activator),
        jnp.where(active, new_inhibitor, inhibitor),
        jnp.where(active, new_tangent_act, tangent_act),
        jnp.where(active, new_tangent_inh, tangent_inh),
    )


def cholesky_kernel(gram, rhs, out_ref):
    size = gram.shape[0]
    tile = gram
    rows = lax.broadcasted_iota(jnp.int32, tile.shape, 0)
    cols = lax.broadcasted_iota(jnp.int32, tile.shape, 1)
    diagonal = rows == cols
    index = rows[:, :1]
    columns = []
    pivots = []
    for outer in range(size):
        value = jnp.sum(jnp.where(cols == outer, tile, 0.0), axis=1, keepdims=True)
        pivot = jnp.sqrt(jnp.sum(jnp.where(index == outer, value, 0.0), axis=0, keepdims=True))
        column = jnp.where(index >= outer, value / pivot, 0.0)
        row = jnp.sum(jnp.where(diagonal, column, 0.0), axis=0, keepdims=True)
        tile = tile - column * row
        columns.append(column)
        pivots.append(pivot)
    accum = -jnp.sum(jnp.where(diagonal, rhs, 0.0), axis=1, keepdims=True)
    middle = jnp.zeros_like(accum)
    for outer in range(size):
        value = jnp.sum(jnp.where(index == outer, accum, 0.0), axis=0, keepdims=True) / pivots[outer]
        middle = jnp.where(index == outer, value, middle)
        accum = accum - columns[outer] * value
    result = jnp.zeros_like(middle)
    for outer in range(size - 1, -1, -1):
        below = jnp.sum(jnp.where(index > outer, columns[outer] * result, 0.0), axis=0, keepdims=True)
        value = jnp.sum(jnp.where(index == outer, middle, 0.0), axis=0, keepdims=True)
        result = jnp.where(index == outer, (value - below) / pivots[outer], result)
    out_ref[0:1, :] = jnp.sum(jnp.where(diagonal, result, 0.0), axis=0, keepdims=True)


def assembly_kernel(jacobian_ref, vectors_ref, out_ref, *, total):
    vectors = vectors_ref[...]
    lanes = lax.broadcasted_iota(jnp.int32, (1, vectors.shape[1]), 1)
    gap_sum = jnp.sum(jnp.where(lanes == 0, vectors[2:3], 0.0), axis=1, keepdims=True)
    mismatch_sum = jnp.sum(jnp.where(lanes == 1, vectors[2:3], 0.0), axis=1, keepdims=True)
    distance = gap_sum / total + SMALL_EPSILON
    deflator = 1.0 / distance + 1.0
    slopes_row = -2.0 * (vectors[0:1] / total) / (distance * distance)
    cross_row = vectors[1:2]
    tile = jacobian_ref[...]
    rows = lax.broadcasted_iota(jnp.int32, tile.shape, 0)
    cols = lax.broadcasted_iota(jnp.int32, tile.shape, 1)
    diagonal = rows == cols
    slopes_col = jnp.sum(jnp.where(diagonal, slopes_row, 0.0), axis=1, keepdims=True)
    cross_col = jnp.sum(jnp.where(diagonal, cross_row, 0.0), axis=1, keepdims=True)
    gram = (
        deflator * deflator * tile
        + deflator * slopes_col * cross_row
        + deflator * cross_col * slopes_row
        + slopes_col * slopes_row * mismatch_sum
    ) / total
    rhs = (deflator * deflator * cross_row + deflator * slopes_row * mismatch_sum) / total
    cholesky_kernel(gram, rhs, out_ref)
    out_ref[1:2, :] = jnp.broadcast_to(deflator, rhs.shape)


def solve_small(jacobian_sum, along_sum, cross_sum, gap_sum, mismatch_sum, total):
    size = jacobian_sum.shape[0]
    lanes = 128
    padded = jnp.pad(jacobian_sum, ((0, 0), (0, lanes - size)))
    scalars = jnp.stack([gap_sum, mismatch_sum])
    vectors = jnp.stack(
        [
            jnp.pad(along_sum, (0, lanes - size)),
            jnp.pad(cross_sum, (0, lanes - size)),
            jnp.pad(scalars, (0, lanes - 2)),
        ],
        0,
    )
    out = pl.pallas_call(
        functools.partial(assembly_kernel, total=total),
        out_shape=jax.ShapeDtypeStruct((2, lanes), jnp.float32),
    )(padded, vectors)
    return out[0, :size], out[1, 0]


def on_device(state, panel, region, feed_table, step_counts):
    start = state[0, 0]
    row_count = start.shape[1]
    column_count = start.shape[2]
    directions = panel.shape[2]
    tangent = panel[0, 0].reshape(2 * directions, row_count, column_count)
    stacked = jnp.concatenate([start, tangent], 0)
    following = passed_along(stacked, "tm", -1)
    partner_state = swapped(start, "branch", 0)
    classes = jnp.arange(feed_table.shape[0], dtype=jnp.int32)
    feed_rate = jnp.sum(
        jnp.where(region[None] == classes[:, None, None], feed_table[:, None, None], 0.0), 0
    )
    step_limit = step_counts[0]
    panel_rows = panel[0, 0].reshape(directions, -1)
    gap = (start - partner_state).reshape(-1)
    total = 2.0 * lax.axis_size("tm") * row_count * lax.axis_size(SPACE) * column_count
    gap_part = jnp.sum(gap * gap)
    along_part = jnp.sum(panel_rows * gap[None, :], 1)
    first_sum = jnp.concatenate([gap_part[None], along_part])
    widened = extended_2(jnp.concatenate([stacked, feed_rate[None]], 0), ((SPACE, 1),), STEPS)
    fields = (widened[0], widened[1], widened[2:-1:2], widened[3:-1:2])
    feed_wide = widened[-1]
    total_rows = feed_wide.shape[0]
    for step_index in range(STEPS):
        fields = advance(
            fields,
            feed_wide[step_index + 1 : total_rows - step_index - 1],
            step_index < step_limit,
        )
    end_state = jnp.stack(fields[:2], 0)
    end_tangent = jnp.stack(fields[2:], 1).reshape(directions, -1)
    arrived = passed_along(end_state, "tm", 1)
    next_mismatch = (end_state - following[:2]).reshape(-1)
    next_jacobian = end_tangent - following[2:].reshape(directions, -1)
    jacobian_gram = jnp.dot(next_jacobian, next_jacobian.T, precision=HIGH)
    jacobian_mismatch = jnp.sum(next_jacobian * next_mismatch[None, :], 1)
    mismatch_square = jnp.sum(next_mismatch * next_mismatch)
    moments = one_axis_at_a_time(
        jnp.concatenate(
            [first_sum, mismatch_square[None], jacobian_mismatch, jacobian_gram.reshape(-1)]
        ),
        TM_SPACE,
    )
    gap_sum = moments[0]
    along_sum = moments[1 : 1 + directions]
    mismatch_sum = moments[1 + directions]
    cross_sum = moments[2 + directions : 2 + 2 * directions]
    jacobian_sum = moments[2 + 2 * directions :].reshape(directions, directions)
    coefficients, deflator = solve_small(
        jacobian_sum, along_sum, cross_sum, gap_sum, mismatch_sum, total
    )
    mismatch = (arrived - start).reshape(-1)
    deflated = deflator * mismatch
    correction = jnp.sum(coefficients[:, None, None, None] * panel[0, 0], 0)
    return (
        deflated.reshape(1, 1, 2, row_count, column_count),
        correction.reshape(1, 1, 2, row_count, column_count),
        coefficients.reshape(1, directions),
    )


def solution(mesh):
    finer = Mesh(
        mesh.devices.reshape(mesh.shape["tm"], 4, 4, mesh.shape["branch"]),
        ("tm", "space_0", "space_1", "branch"),
    )
    in_specs = (
        P("branch", "tm", None, SPACE, None),
        P("branch", "tm", None, None, SPACE, None),
        P(SPACE, None),
        P(),
        P("tm"),
    )
    out_specs = (
        P("branch", "tm", None, SPACE, None),
        P("branch", "tm", None, SPACE, None),
        P("branch", None),
    )
    return jax.shard_map(
        on_device, mesh=finer, in_specs=in_specs, out_specs=out_specs, check_vma=False
    )
```

```python
import functools

import jax
import jax.numpy as jnp
from jax import lax
from jax.sharding import Mesh
from jax.sharding import PartitionSpec as P
from jax.experimental import pallas as pl

STEPS = 5
SPACE = ("space_0", "space_1")
TM_SPACE = ("tm", "space_0", "space_1")


TIME_STEP = 0.03
ACTIVATOR_DIFFUSION = 1.0
INHIBITOR_DIFFUSION = 6.0
REACTION_RATE = 2.5
SMALL_EPSILON = 1e-06
HIGHEST = lax.Precision.HIGHEST
HIGH = lax.Precision.HIGH


def extended_2(cells, sides, width):
    for axis, dim in sides:
        count = lax.axis_size(axis)
        head = lax.slice_in_dim(cells, 0, width, axis=dim)
        tail = lax.slice_in_dim(cells, cells.shape[dim] - width, cells.shape[dim], axis=dim)
        cells = jnp.concatenate(
            [
                lax.ppermute(tail, axis, [(i, (i + 1) % count) for i in range(count)]),
                cells,
                lax.ppermute(head, axis, [((i + 1) % count, i) for i in range(count)]),
            ],
            axis=dim,
        )
    return cells


def swapped(value, axis, apart):
    mask = 2**apart
    pairs = [(source, source ^ mask) for source in range(lax.axis_size(axis))]
    return lax.ppermute(value, axis, pairs)


def passed_along(block, axis, distance):
    devices = range(lax.axis_size(axis))
    route = [((i - distance) % len(devices), i) for i in devices]
    return lax.ppermute(block, axis, route)


def butterfly_rounds(axes):
    rounds = []
    for axis in axes:
        count = lax.axis_size(axis)
        apart = 1
        while apart < count:
            rounds.append((axis, [(i, i ^ apart) for i in range(count)]))
            apart *= 2
    return rounds


def one_axis_at_a_time(x, axes):
    for axis, pairs in butterfly_rounds(axes):
        x = x + lax.ppermute(x, axis, pairs)
    return x


def laplacian_rows(extended):
    interior = extended[..., 1:-1, :]
    return (
        extended[..., 2:, :]
        + extended[..., :-2, :]
        + jnp.roll(interior, 1, -1)
        + jnp.roll(interior, -1, -1)
        - 4.0 * interior
    )


def advance(fields, feed_rate, active):
    activator_wide, inhibitor_wide, tangent_act_wide, tangent_inh_wide = fields
    activator = activator_wide[1:-1]
    inhibitor = inhibitor_wide[1:-1]
    tangent_act = tangent_act_wide[:, 1:-1]
    tangent_inh = tangent_inh_wide[:, 1:-1]
    squared = activator * activator
    product = activator * inhibitor
    new_activator = activator + TIME_STEP * (
        ACTIVATOR_DIFFUSION * laplacian_rows(activator_wide)
        + feed_rate
        - (REACTION_RATE + 1.0) * activator
        + squared * inhibitor
    )
    new_inhibitor = inhibitor + TIME_STEP * (
        INHIBITOR_DIFFUSION * laplacian_rows(inhibitor_wide)
        + REACTION_RATE * activator
        - squared * inhibitor
    )
    new_tangent_act = tangent_act + TIME_STEP * (
        ACTIVATOR_DIFFUSION * laplacian_rows(tangent_act_wide)
        + (2.0 * product - REACTION_RATE - 1.0) * tangent_act
        + squared * tangent_inh
    )
    new_tangent_inh = tangent_inh + TIME_STEP * (
        INHIBITOR_DIFFUSION * laplacian_rows(tangent_inh_wide)
        + (REACTION_RATE - 2.0 * product) * tangent_act
        - squared * tangent_inh
    )
    return (
        jnp.where(active, new_activator, activator),
        jnp.where(active, new_inhibitor, inhibitor),
        jnp.where(active, new_tangent_act, tangent_act),
        jnp.where(active, new_tangent_inh, tangent_inh),
    )


def cholesky_kernel(gram, rhs, out_ref):
    size = gram.shape[0]
    tile = gram
    rows = lax.broadcasted_iota(jnp.int32, tile.shape, 0)
    cols = lax.broadcasted_iota(jnp.int32, tile.shape, 1)
    diagonal = rows == cols
    index = rows[:, :1]
    columns = []
    pivots = []
    for outer in range(size):
        value = jnp.sum(jnp.where(cols == outer, tile, 0.0), axis=1, keepdims=True)
        pivot = jnp.sqrt(jnp.sum(jnp.where(index == outer, value, 0.0), axis=0, keepdims=True))
        column = jnp.where(index >= outer, value / pivot, 0.0)
        row = jnp.sum(jnp.where(diagonal, column, 0.0), axis=0, keepdims=True)
        tile = tile - column * row
        columns.append(column)
        pivots.append(pivot)
    accum = -jnp.sum(jnp.where(diagonal, rhs, 0.0), axis=1, keepdims=True)
    middle = jnp.zeros_like(accum)
    for outer in range(size):
        value = jnp.sum(jnp.where(index == outer, accum, 0.0), axis=0, keepdims=True) / pivots[outer]
        middle = jnp.where(index == outer, value, middle)
        accum = accum - columns[outer] * value
    result = jnp.zeros_like(middle)
    for outer in range(size - 1, -1, -1):
        below = jnp.sum(jnp.where(index > outer, columns[outer] * result, 0.0), axis=0, keepdims=True)
        value = jnp.sum(jnp.where(index == outer, middle, 0.0), axis=0, keepdims=True)
        result = jnp.where(index == outer, (value - below) / pivots[outer], result)
    out_ref[...] = jnp.sum(jnp.where(diagonal, result, 0.0), axis=0, keepdims=True)[:, :size]


def assembly_kernel(jacobian_ref, vectors_ref, out_ref, deflator_ref, *, total):
    vectors = vectors_ref[...]
    lanes = lax.broadcasted_iota(jnp.int32, (1, vectors.shape[1]), 1)
    gap_sum = jnp.sum(jnp.where(lanes == 0, vectors[2:3], 0.0), axis=1, keepdims=True)
    mismatch_sum = jnp.sum(jnp.where(lanes == 1, vectors[2:3], 0.0), axis=1, keepdims=True)
    distance = gap_sum / total + SMALL_EPSILON
    deflator = 1.0 / distance + 1.0
    slopes_row = -2.0 * (vectors[0:1] / total) / (distance * distance)
    cross_row = vectors[1:2]
    tile = jacobian_ref[...]
    rows = lax.broadcasted_iota(jnp.int32, tile.shape, 0)
    cols = lax.broadcasted_iota(jnp.int32, tile.shape, 1)
    diagonal = rows == cols
    slopes_col = jnp.sum(jnp.where(diagonal, slopes_row, 0.0), axis=1, keepdims=True)
    cross_col = jnp.sum(jnp.where(diagonal, cross_row, 0.0), axis=1, keepdims=True)
    gram = (
        deflator * deflator * tile
        + deflator * slopes_col * cross_row
        + deflator * cross_col * slopes_row
        + slopes_col * slopes_row * mismatch_sum
    ) / total
    rhs = (deflator * deflator * cross_row + deflator * slopes_row * mismatch_sum) / total
    cholesky_kernel(gram, rhs, out_ref)
    deflator_ref[...] = deflator


def solve_small(jacobian_sum, along_sum, cross_sum, gap_sum, mismatch_sum, total):
    size = jacobian_sum.shape[0]
    lanes = 128
    padded = jnp.pad(jacobian_sum, ((0, 0), (0, lanes - size)))
    scalars = jnp.stack([gap_sum, mismatch_sum])
    vectors = jnp.stack(
        [
            jnp.pad(along_sum, (0, lanes - size)),
            jnp.pad(cross_sum, (0, lanes - size)),
            jnp.pad(scalars, (0, lanes - 2)),
        ],
        0,
    )
    return pl.pallas_call(
        functools.partial(assembly_kernel, total=total),
        out_shape=(
            jax.ShapeDtypeStruct((1, size), jnp.float32),
            jax.ShapeDtypeStruct((1, 1), jnp.float32),
        ),
    )(padded, vectors)


def on_device(state, panel, region, feed_table, step_counts):
    start = state[0, 0]
    row_count = start.shape[1]
    column_count = start.shape[2]
    directions = panel.shape[2]
    tangent = panel[0, 0].reshape(2 * directions, row_count, column_count)
    stacked = jnp.concatenate([start, tangent], 0)
    following = passed_along(stacked, "tm", -1)
    partner_state = swapped(start, "branch", 0)
    classes = jnp.arange(feed_table.shape[0], dtype=jnp.int32)
    feed_rate = jnp.sum(
        jnp.where(region[None] == classes[:, None, None], feed_table[:, None, None], 0.0), 0
    )
    step_limit = step_counts[0]
    panel_rows = panel[0, 0].reshape(directions, -1)
    gap = (start - partner_state).reshape(-1)
    total = 2.0 * lax.axis_size("tm") * row_count * lax.axis_size(SPACE) * column_count
    gap_part = jnp.sum(gap * gap)
    along_part = jnp.sum(panel_rows * gap[None, :], 1)
    first_sum = jnp.concatenate([gap_part[None], along_part])
    widened = extended_2(jnp.concatenate([stacked, feed_rate[None]], 0), ((SPACE, 1),), STEPS)
    fields = (widened[0], widened[1], widened[2:-1:2], widened[3:-1:2])
    feed_wide = widened[-1]
    total_rows = feed_wide.shape[0]
    for step_index in range(STEPS):
        fields = advance(
            fields,
            feed_wide[step_index + 1 : total_rows - step_index - 1],
            step_index < step_limit,
        )
    end_state = jnp.stack(fields[:2], 0)
    end_tangent = jnp.stack(fields[2:], 1).reshape(directions, -1)
    arrived = passed_along(end_state, "tm", 1)
    next_mismatch = (end_state - following[:2]).reshape(-1)
    next_jacobian = end_tangent - following[2:].reshape(directions, -1)
    jacobian_gram = jnp.dot(next_jacobian, next_jacobian.T, precision=HIGH)
    jacobian_mismatch = jnp.sum(next_jacobian * next_mismatch[None, :], 1)
    mismatch_square = jnp.sum(next_mismatch * next_mismatch)
    moments = one_axis_at_a_time(
        jnp.concatenate(
            [first_sum, mismatch_square[None], jacobian_mismatch, jacobian_gram.reshape(-1)]
        ),
        TM_SPACE,
    )
    gap_sum = moments[0]
    along_sum = moments[1 : 1 + directions]
    mismatch_sum = moments[1 + directions]
    cross_sum = moments[2 + directions : 2 + 2 * directions]
    jacobian_sum = moments[2 + 2 * directions :].reshape(directions, directions)
    coefficients, deflator = solve_small(
        jacobian_sum, along_sum, cross_sum, gap_sum, mismatch_sum, total
    )
    mismatch = (arrived - start).reshape(-1)
    deflated = deflator.reshape(()) * mismatch
    correction = jnp.sum(coefficients.reshape(directions, 1, 1, 1) * panel[0, 0], 0)
    return (
        deflated.reshape(1, 1, 2, row_count, column_count),
        correction.reshape(1, 1, 2, row_count, column_count),
        coefficients.reshape(1, directions),
    )


def solution(mesh):
    finer = Mesh(
        mesh.devices.reshape(mesh.shape["tm"], 4, 4, mesh.shape["branch"]),
        ("tm", "space_0", "space_1", "branch"),
    )
    in_specs = (
        P("branch", "tm", None, SPACE, None),
        P("branch", "tm", None, None, SPACE, None),
        P(SPACE, None),
        P(),
        P("tm"),
    )
    out_specs = (
        P("branch", "tm", None, SPACE, None),
        P("branch", "tm", None, SPACE, None),
        P("branch", None),
    )
    return jax.shard_map(
        on_device, mesh=finer, in_specs=in_specs, out_specs=out_specs, check_vma=False
    )
```

```python
import functools

import jax
import jax.numpy as jnp
from jax import lax
from jax.sharding import Mesh
from jax.sharding import PartitionSpec as P
from jax.experimental import pallas as pl

STEPS = 5
SPACE = ("space_0", "space_1")
TM_SPACE = ("tm", "space_0", "space_1")


TIME_STEP = 0.03
ACTIVATOR_DIFFUSION = 1.0
INHIBITOR_DIFFUSION = 6.0
REACTION_RATE = 2.5
SMALL_EPSILON = 1e-06
HIGHEST = lax.Precision.HIGHEST
HIGH = lax.Precision.HIGH


def extended_2(cells, sides, width):
    for axis, dim in sides:
        count = lax.axis_size(axis)
        head = lax.slice_in_dim(cells, 0, width, axis=dim)
        tail = lax.slice_in_dim(cells, cells.shape[dim] - width, cells.shape[dim], axis=dim)
        cells = jnp.concatenate(
            [
                lax.ppermute(tail, axis, [(i, (i + 1) % count) for i in range(count)]),
                cells,
                lax.ppermute(head, axis, [((i + 1) % count, i) for i in range(count)]),
            ],
            axis=dim,
        )
    return cells


def swapped(value, axis, apart):
    mask = 2**apart
    pairs = [(source, source ^ mask) for source in range(lax.axis_size(axis))]
    return lax.ppermute(value, axis, pairs)


def passed_along(block, axis, distance):
    devices = range(lax.axis_size(axis))
    route = [((i - distance) % len(devices), i) for i in devices]
    return lax.ppermute(block, axis, route)


def butterfly_rounds(axes):
    rounds = []
    for axis in axes:
        count = lax.axis_size(axis)
        apart = 1
        while apart < count:
            rounds.append((axis, [(i, i ^ apart) for i in range(count)]))
            apart *= 2
    return rounds


def one_axis_at_a_time(x, axes):
    for axis, pairs in butterfly_rounds(axes):
        x = x + lax.ppermute(x, axis, pairs)
    return x


def laplacian_rows(extended):
    interior = extended[..., 1:-1, :]
    return (
        extended[..., 2:, :]
        + extended[..., :-2, :]
        + jnp.roll(interior, 1, -1)
        + jnp.roll(interior, -1, -1)
        - 4.0 * interior
    )


def advance(fields, feed_rate, active):
    activator_wide, inhibitor_wide, tangent_act_wide, tangent_inh_wide = fields
    activator = activator_wide[1:-1]
    inhibitor = inhibitor_wide[1:-1]
    tangent_act = tangent_act_wide[:, 1:-1]
    tangent_inh = tangent_inh_wide[:, 1:-1]
    squared = activator * activator
    product = activator * inhibitor
    new_activator = activator + TIME_STEP * (
        ACTIVATOR_DIFFUSION * laplacian_rows(activator_wide)
        + feed_rate
        - (REACTION_RATE + 1.0) * activator
        + squared * inhibitor
    )
    new_inhibitor = inhibitor + TIME_STEP * (
        INHIBITOR_DIFFUSION * laplacian_rows(inhibitor_wide)
        + REACTION_RATE * activator
        - squared * inhibitor
    )
    new_tangent_act = tangent_act + TIME_STEP * (
        ACTIVATOR_DIFFUSION * laplacian_rows(tangent_act_wide)
        + (2.0 * product - REACTION_RATE - 1.0) * tangent_act
        + squared * tangent_inh
    )
    new_tangent_inh = tangent_inh + TIME_STEP * (
        INHIBITOR_DIFFUSION * laplacian_rows(tangent_inh_wide)
        + (REACTION_RATE - 2.0 * product) * tangent_act
        - squared * tangent_inh
    )
    return (
        jnp.where(active, new_activator, activator),
        jnp.where(active, new_inhibitor, inhibitor),
        jnp.where(active, new_tangent_act, tangent_act),
        jnp.where(active, new_tangent_inh, tangent_inh),
    )


def cholesky_kernel(gram, rhs, out_ref):
    size = gram.shape[0]
    tile = gram
    rows = lax.broadcasted_iota(jnp.int32, tile.shape, 0)
    cols = lax.broadcasted_iota(jnp.int32, tile.shape, 1)
    diagonal = rows == cols
    index = rows[:, :1]
    columns = []
    pivots = []
    for outer in range(size):
        value = jnp.sum(jnp.where(cols == outer, tile, 0.0), axis=1, keepdims=True)
        pivot = jnp.sqrt(jnp.sum(jnp.where(index == outer, value, 0.0), axis=0, keepdims=True))
        column = jnp.where(index >= outer, value / pivot, 0.0)
        row = jnp.sum(jnp.where(diagonal, column, 0.0), axis=0, keepdims=True)
        tile = tile - column * row
        columns.append(column)
        pivots.append(pivot)
    accum = -jnp.sum(jnp.where(diagonal, rhs, 0.0), axis=1, keepdims=True)
    middle = jnp.zeros_like(accum)
    for outer in range(size):
        value = jnp.sum(jnp.where(index == outer, accum, 0.0), axis=0, keepdims=True) / pivots[outer]
        middle = jnp.where(index == outer, value, middle)
        accum = accum - columns[outer] * value
    result = jnp.zeros_like(middle)
    for outer in range(size - 1, -1, -1):
        below = jnp.sum(jnp.where(index > outer, columns[outer] * result, 0.0), axis=0, keepdims=True)
        value = jnp.sum(jnp.where(index == outer, middle, 0.0), axis=0, keepdims=True)
        result = jnp.where(index == outer, (value - below) / pivots[outer], result)
    out_ref[...] = jnp.sum(jnp.where(diagonal, result, 0.0), axis=0, keepdims=True)[:, :size]


def assembly_kernel(jacobian_ref, along_ref, cross_ref, scalar_ref, out_ref, deflator_ref, *, total):
    scalars = scalar_ref[...]
    gap_sum = scalars[:, 0:1]
    mismatch_sum = scalars[:, 1:2]
    distance = gap_sum / total + SMALL_EPSILON
    deflator = 1.0 / distance + 1.0
    slopes_row = -2.0 * (along_ref[...] / total) / (distance * distance)
    cross_row = cross_ref[...]
    tile = jacobian_ref[...]
    rows = lax.broadcasted_iota(jnp.int32, tile.shape, 0)
    cols = lax.broadcasted_iota(jnp.int32, tile.shape, 1)
    diagonal = rows == cols
    slopes_col = jnp.sum(jnp.where(diagonal, slopes_row, 0.0), axis=1, keepdims=True)
    cross_col = jnp.sum(jnp.where(diagonal, cross_row, 0.0), axis=1, keepdims=True)
    gram = (
        deflator * deflator * tile
        + deflator * slopes_col * cross_row
        + deflator * cross_col * slopes_row
        + slopes_col * slopes_row * mismatch_sum
    ) / total
    rhs = (deflator * deflator * cross_row + deflator * slopes_row * mismatch_sum) / total
    cholesky_kernel(gram, rhs, out_ref)
    deflator_ref[...] = deflator


def solve_small(jacobian_sum, along_sum, cross_sum, scalars, total):
    size = jacobian_sum.shape[0]
    return pl.pallas_call(
        functools.partial(assembly_kernel, total=total),
        out_shape=(
            jax.ShapeDtypeStruct((1, size), jnp.float32),
            jax.ShapeDtypeStruct((1, 1), jnp.float32),
        ),
    )(jacobian_sum, along_sum.reshape(1, size), cross_sum.reshape(1, size), scalars.reshape(1, 2))


def on_device(state, panel, region, feed_table, step_counts):
    start = state[0, 0]
    row_count = start.shape[1]
    column_count = start.shape[2]
    directions = panel.shape[2]
    tangent = panel[0, 0].reshape(2 * directions, row_count, column_count)
    stacked = jnp.concatenate([start, tangent], 0)
    following = passed_along(stacked, "tm", -1)
    partner_state = swapped(start, "branch", 0)
    classes = jnp.arange(feed_table.shape[0], dtype=jnp.int32)
    feed_rate = jnp.sum(
        jnp.where(region[None] == classes[:, None, None], feed_table[:, None, None], 0.0), 0
    )
    step_limit = step_counts[0]
    panel_rows = panel[0, 0].reshape(directions, -1)
    gap = (start - partner_state).reshape(-1)
    total = 2.0 * lax.axis_size("tm") * row_count * lax.axis_size(SPACE) * column_count
    gap_part = jnp.sum(gap * gap)
    along_part = jnp.sum(panel_rows * gap[None, :], 1)
    widened = extended_2(jnp.concatenate([stacked, feed_rate[None]], 0), ((SPACE, 1),), STEPS)
    fields = (widened[0], widened[1], widened[2:-1:2], widened[3:-1:2])
    feed_wide = widened[-1]
    total_rows = feed_wide.shape[0]
    for step_index in range(STEPS):
        fields = advance(
            fields,
            feed_wide[step_index + 1 : total_rows - step_index - 1],
            step_index < step_limit,
        )
    end_state = jnp.stack(fields[:2], 0)
    end_tangent = jnp.stack(fields[2:], 1).reshape(directions, -1)
    arrived = passed_along(end_state, "tm", 1)
    next_mismatch = (end_state - following[:2]).reshape(-1)
    next_jacobian = end_tangent - following[2:].reshape(directions, -1)
    jacobian_gram = jnp.dot(next_jacobian, next_jacobian.T, precision=HIGH)
    jacobian_mismatch = jnp.sum(next_jacobian * next_mismatch[None, :], 1)
    mismatch_square = jnp.sum(next_mismatch * next_mismatch)
    moments = one_axis_at_a_time(
        jnp.concatenate(
            [
                gap_part[None],
                mismatch_square[None],
                along_part,
                jacobian_mismatch,
                jacobian_gram.reshape(-1),
            ]
        ),
        TM_SPACE,
    )
    scalars = moments[:2]
    along_sum = moments[2 : 2 + directions]
    cross_sum = moments[2 + directions : 2 + 2 * directions]
    jacobian_sum = moments[2 + 2 * directions :].reshape(directions, directions)
    coefficients, deflator = solve_small(jacobian_sum, along_sum, cross_sum, scalars, total)
    mismatch = (arrived - start).reshape(-1)
    deflated = deflator.reshape(()) * mismatch
    correction = jnp.sum(coefficients.reshape(directions, 1, 1, 1) * panel[0, 0], 0)
    return (
        deflated.reshape(1, 1, 2, row_count, column_count),
        correction.reshape(1, 1, 2, row_count, column_count),
        coefficients.reshape(1, directions),
    )


def solution(mesh):
    finer = Mesh(
        mesh.devices.reshape(mesh.shape["tm"], 4, 4, mesh.shape["branch"]),
        ("tm", "space_0", "space_1", "branch"),
    )
    in_specs = (
        P("branch", "tm", None, SPACE, None),
        P("branch", "tm", None, None, SPACE, None),
        P(SPACE, None),
        P(),
        P("tm"),
    )
    out_specs = (
        P("branch", "tm", None, SPACE, None),
        P("branch", "tm", None, SPACE, None),
        P("branch", None),
    )
    return jax.shard_map(
        on_device, mesh=finer, in_specs=in_specs, out_specs=out_specs, check_vma=False
    )
```

```python
import functools

import jax
import jax.numpy as jnp
from jax import lax
from jax.sharding import Mesh
from jax.sharding import PartitionSpec as P
from jax.experimental import pallas as pl

STEPS = 5
SPACE = ("space_0", "space_1")
TM_SPACE = ("tm", "space_0", "space_1")


TIME_STEP = 0.03
ACTIVATOR_DIFFUSION = 1.0
INHIBITOR_DIFFUSION = 6.0
REACTION_RATE = 2.5
SMALL_EPSILON = 1e-06
HIGHEST = lax.Precision.HIGHEST
HIGH = lax.Precision.HIGH


def extended_2(cells, sides, width):
    for axis, dim in sides:
        count = lax.axis_size(axis)
        head = lax.slice_in_dim(cells, 0, width, axis=dim)
        tail = lax.slice_in_dim(cells, cells.shape[dim] - width, cells.shape[dim], axis=dim)
        cells = jnp.concatenate(
            [
                lax.ppermute(tail, axis, [(i, (i + 1) % count) for i in range(count)]),
                cells,
                lax.ppermute(head, axis, [((i + 1) % count, i) for i in range(count)]),
            ],
            axis=dim,
        )
    return cells


def swapped(value, axis, apart):
    mask = 2**apart
    pairs = [(source, source ^ mask) for source in range(lax.axis_size(axis))]
    return lax.ppermute(value, axis, pairs)


def passed_along(block, axis, distance):
    devices = range(lax.axis_size(axis))
    route = [((i - distance) % len(devices), i) for i in devices]
    return lax.ppermute(block, axis, route)


def butterfly_rounds(axes):
    rounds = []
    for axis in axes:
        count = lax.axis_size(axis)
        apart = 1
        while apart < count:
            rounds.append((axis, [(i, i ^ apart) for i in range(count)]))
            apart *= 2
    return rounds


def one_axis_at_a_time(x, axes):
    for axis, pairs in butterfly_rounds(axes):
        x = x + lax.ppermute(x, axis, pairs)
    return x


def laplacian_rows(extended):
    interior = extended[..., 1:-1, :]
    return (
        extended[..., 2:, :]
        + extended[..., :-2, :]
        + jnp.roll(interior, 1, -1)
        + jnp.roll(interior, -1, -1)
        - 4.0 * interior
    )


def advance(fields, feed_rate, active):
    activator_wide, inhibitor_wide, tangent_act_wide, tangent_inh_wide = fields
    activator = activator_wide[1:-1]
    inhibitor = inhibitor_wide[1:-1]
    tangent_act = tangent_act_wide[:, 1:-1]
    tangent_inh = tangent_inh_wide[:, 1:-1]
    squared = activator * activator
    product = activator * inhibitor
    new_activator = activator + TIME_STEP * (
        ACTIVATOR_DIFFUSION * laplacian_rows(activator_wide)
        + feed_rate
        - (REACTION_RATE + 1.0) * activator
        + squared * inhibitor
    )
    new_inhibitor = inhibitor + TIME_STEP * (
        INHIBITOR_DIFFUSION * laplacian_rows(inhibitor_wide)
        + REACTION_RATE * activator
        - squared * inhibitor
    )
    new_tangent_act = tangent_act + TIME_STEP * (
        ACTIVATOR_DIFFUSION * laplacian_rows(tangent_act_wide)
        + (2.0 * product - REACTION_RATE - 1.0) * tangent_act
        + squared * tangent_inh
    )
    new_tangent_inh = tangent_inh + TIME_STEP * (
        INHIBITOR_DIFFUSION * laplacian_rows(tangent_inh_wide)
        + (REACTION_RATE - 2.0 * product) * tangent_act
        - squared * tangent_inh
    )
    return (
        jnp.where(active, new_activator, activator),
        jnp.where(active, new_inhibitor, inhibitor),
        jnp.where(active, new_tangent_act, tangent_act),
        jnp.where(active, new_tangent_inh, tangent_inh),
    )


def cholesky_kernel(gram, rhs, out_ref):
    size = gram.shape[0]
    tile = gram
    rows = lax.broadcasted_iota(jnp.int32, tile.shape, 0)
    cols = lax.broadcasted_iota(jnp.int32, tile.shape, 1)
    diagonal = rows == cols
    index = rows[:, :1]
    columns = []
    pivots = []
    for outer in range(size):
        value = jnp.sum(jnp.where(cols == outer, tile, 0.0), axis=1, keepdims=True)
        pivot = jnp.sqrt(jnp.sum(jnp.where(index == outer, value, 0.0), axis=0, keepdims=True))
        column = jnp.where(index >= outer, value / pivot, 0.0)
        row = jnp.sum(jnp.where(diagonal, column, 0.0), axis=0, keepdims=True)
        tile = tile - column * row
        columns.append(column)
        pivots.append(pivot)
    accum = -jnp.sum(jnp.where(diagonal, rhs, 0.0), axis=1, keepdims=True)
    middle = jnp.zeros_like(accum)
    for outer in range(size):
        value = jnp.sum(jnp.where(index == outer, accum, 0.0), axis=0, keepdims=True) / pivots[outer]
        middle = jnp.where(index == outer, value, middle)
        accum = accum - columns[outer] * value
    result = jnp.zeros_like(middle)
    for outer in range(size - 1, -1, -1):
        below = jnp.sum(jnp.where(index > outer, columns[outer] * result, 0.0), axis=0, keepdims=True)
        value = jnp.sum(jnp.where(index == outer, middle, 0.0), axis=0, keepdims=True)
        result = jnp.where(index == outer, (value - below) / pivots[outer], result)
    out_ref[...] = jnp.sum(jnp.where(diagonal, result, 0.0), axis=0, keepdims=True)[:, :size]


def assembly_kernel(moments_ref, out_ref, deflator_ref, *, total):
    size = moments_ref.shape[1]
    scalars = moments_ref[size + 2 : size + 3, :]
    gap_sum = scalars[:, 0:1]
    mismatch_sum = scalars[:, 1:2]
    distance = gap_sum / total + SMALL_EPSILON
    deflator = 1.0 / distance + 1.0
    slopes_row = -2.0 * (moments_ref[size + 1 : size + 2, :] / total) / (distance * distance)
    cross_row = moments_ref[size : size + 1, :]
    tile = moments_ref[0:size, :]
    rows = lax.broadcasted_iota(jnp.int32, tile.shape, 0)
    cols = lax.broadcasted_iota(jnp.int32, tile.shape, 1)
    diagonal = rows == cols
    slopes_col = jnp.sum(jnp.where(diagonal, slopes_row, 0.0), axis=1, keepdims=True)
    cross_col = jnp.sum(jnp.where(diagonal, cross_row, 0.0), axis=1, keepdims=True)
    gram = (
        deflator * deflator * tile
        + deflator * slopes_col * cross_row
        + deflator * cross_col * slopes_row
        + slopes_col * slopes_row * mismatch_sum
    ) / total
    rhs = (deflator * deflator * cross_row + deflator * slopes_row * mismatch_sum) / total
    cholesky_kernel(gram, rhs, out_ref)
    deflator_ref[...] = deflator


def solve_small(moments, total):
    size = moments.shape[1]
    return pl.pallas_call(
        functools.partial(assembly_kernel, total=total),
        out_shape=(
            jax.ShapeDtypeStruct((1, size), jnp.float32),
            jax.ShapeDtypeStruct((1, 1), jnp.float32),
        ),
    )(moments)


def on_device(state, panel, region, feed_table, step_counts):
    start = state[0, 0]
    row_count = start.shape[1]
    column_count = start.shape[2]
    directions = panel.shape[2]
    tangent = panel[0, 0].reshape(2 * directions, row_count, column_count)
    stacked = jnp.concatenate([start, tangent], 0)
    following = passed_along(stacked, "tm", -1)
    partner_state = swapped(start, "branch", 0)
    classes = jnp.arange(feed_table.shape[0], dtype=jnp.int32)
    feed_rate = jnp.sum(
        jnp.where(region[None] == classes[:, None, None], feed_table[:, None, None], 0.0), 0
    )
    step_limit = step_counts[0]
    panel_rows = panel[0, 0].reshape(directions, -1)
    gap = (start - partner_state).reshape(-1)
    total = 2.0 * lax.axis_size("tm") * row_count * lax.axis_size(SPACE) * column_count
    gap_part = jnp.sum(gap * gap)
    along_part = jnp.sum(panel_rows * gap[None, :], 1)
    widened = extended_2(jnp.concatenate([stacked, feed_rate[None]], 0), ((SPACE, 1),), STEPS)
    fields = (widened[0], widened[1], widened[2:-1:2], widened[3:-1:2])
    feed_wide = widened[-1]
    total_rows = feed_wide.shape[0]
    for step_index in range(STEPS):
        fields = advance(
            fields,
            feed_wide[step_index + 1 : total_rows - step_index - 1],
            step_index < step_limit,
        )
    end_state = jnp.stack(fields[:2], 0)
    end_tangent = jnp.stack(fields[2:], 1).reshape(directions, -1)
    arrived = passed_along(end_state, "tm", 1)
    next_mismatch = (end_state - following[:2]).reshape(-1)
    next_jacobian = end_tangent - following[2:].reshape(directions, -1)
    jacobian_gram = jnp.dot(next_jacobian, next_jacobian.T, precision=HIGH)
    jacobian_mismatch = jnp.sum(next_jacobian * next_mismatch[None, :], 1)
    mismatch_square = jnp.sum(next_mismatch * next_mismatch)
    scalar_row = jnp.zeros((directions,), jnp.float32)
    scalar_row = scalar_row.at[0].set(gap_part).at[1].set(mismatch_square)
    moments = one_axis_at_a_time(
        jnp.concatenate(
            [jacobian_gram, jacobian_mismatch[None], along_part[None], scalar_row[None]], 0
        ),
        TM_SPACE,
    )
    coefficients, deflator = solve_small(moments, total)
    mismatch = (arrived - start).reshape(-1)
    deflated = deflator.reshape(()) * mismatch
    correction = jnp.sum(coefficients.reshape(directions, 1, 1, 1) * panel[0, 0], 0)
    return (
        deflated.reshape(1, 1, 2, row_count, column_count),
        correction.reshape(1, 1, 2, row_count, column_count),
        coefficients.reshape(1, directions),
    )


def solution(mesh):
    finer = Mesh(
        mesh.devices.reshape(mesh.shape["tm"], 4, 4, mesh.shape["branch"]),
        ("tm", "space_0", "space_1", "branch"),
    )
    in_specs = (
        P("branch", "tm", None, SPACE, None),
        P("branch", "tm", None, None, SPACE, None),
        P(SPACE, None),
        P(),
        P("tm"),
    )
    out_specs = (
        P("branch", "tm", None, SPACE, None),
        P("branch", "tm", None, SPACE, None),
        P("branch", None),
    )
    return jax.shard_map(
        on_device, mesh=finer, in_specs=in_specs, out_specs=out_specs, check_vma=False
    )
```

```python
import functools

import jax
import jax.numpy as jnp
from jax import lax
from jax.sharding import Mesh
from jax.sharding import PartitionSpec as P
from jax.experimental import pallas as pl

STEPS = 5
SPACE = ("space_0", "space_1")
TM_SPACE = ("tm", "space_0", "space_1")


TIME_STEP = 0.03
ACTIVATOR_DIFFUSION = 1.0
INHIBITOR_DIFFUSION = 6.0
REACTION_RATE = 2.5
SMALL_EPSILON = 1e-06
HIGHEST = lax.Precision.HIGHEST
HIGH = lax.Precision.HIGH


def extended_2(cells, sides, width):
    for axis, dim in sides:
        count = lax.axis_size(axis)
        head = lax.slice_in_dim(cells, 0, width, axis=dim)
        tail = lax.slice_in_dim(cells, cells.shape[dim] - width, cells.shape[dim], axis=dim)
        cells = jnp.concatenate(
            [
                lax.ppermute(tail, axis, [(i, (i + 1) % count) for i in range(count)]),
                cells,
                lax.ppermute(head, axis, [((i + 1) % count, i) for i in range(count)]),
            ],
            axis=dim,
        )
    return cells


def swapped(value, axis, apart):
    mask = 2**apart
    pairs = [(source, source ^ mask) for source in range(lax.axis_size(axis))]
    return lax.ppermute(value, axis, pairs)


def passed_along(block, axis, distance):
    devices = range(lax.axis_size(axis))
    route = [((i - distance) % len(devices), i) for i in devices]
    return lax.ppermute(block, axis, route)


def butterfly_rounds(axes):
    rounds = []
    for axis in axes:
        count = lax.axis_size(axis)
        apart = 1
        while apart < count:
            rounds.append((axis, [(i, i ^ apart) for i in range(count)]))
            apart *= 2
    return rounds


def one_axis_at_a_time(x, axes):
    for axis, pairs in butterfly_rounds(axes):
        x = x + lax.ppermute(x, axis, pairs)
    return x


def laplacian_rows(extended):
    interior = extended[..., 1:-1, :]
    return (
        extended[..., 2:, :]
        + extended[..., :-2, :]
        + jnp.roll(interior, 1, -1)
        + jnp.roll(interior, -1, -1)
        - 4.0 * interior
    )


def advance(fields, feed_rate, active):
    activator_wide, inhibitor_wide, tangent_act_wide, tangent_inh_wide = fields
    activator = activator_wide[1:-1]
    inhibitor = inhibitor_wide[1:-1]
    tangent_act = tangent_act_wide[:, 1:-1]
    tangent_inh = tangent_inh_wide[:, 1:-1]
    squared = activator * activator
    product = activator * inhibitor
    new_activator = activator + TIME_STEP * (
        ACTIVATOR_DIFFUSION * laplacian_rows(activator_wide)
        + feed_rate
        - (REACTION_RATE + 1.0) * activator
        + squared * inhibitor
    )
    new_inhibitor = inhibitor + TIME_STEP * (
        INHIBITOR_DIFFUSION * laplacian_rows(inhibitor_wide)
        + REACTION_RATE * activator
        - squared * inhibitor
    )
    new_tangent_act = tangent_act + TIME_STEP * (
        ACTIVATOR_DIFFUSION * laplacian_rows(tangent_act_wide)
        + (2.0 * product - REACTION_RATE - 1.0) * tangent_act
        + squared * tangent_inh
    )
    new_tangent_inh = tangent_inh + TIME_STEP * (
        INHIBITOR_DIFFUSION * laplacian_rows(tangent_inh_wide)
        + (REACTION_RATE - 2.0 * product) * tangent_act
        - squared * tangent_inh
    )
    return (
        jnp.where(active, new_activator, activator),
        jnp.where(active, new_inhibitor, inhibitor),
        jnp.where(active, new_tangent_act, tangent_act),
        jnp.where(active, new_tangent_inh, tangent_inh),
    )


def cholesky_kernel(gram, rhs, out_ref):
    size = gram.shape[0]
    tile = gram
    rows = lax.broadcasted_iota(jnp.int32, tile.shape, 0)
    cols = lax.broadcasted_iota(jnp.int32, tile.shape, 1)
    diagonal = rows == cols
    index = rows[:, :1]
    columns = []
    pivots = []
    for outer in range(size):
        value = jnp.sum(jnp.where(cols == outer, tile, 0.0), axis=1, keepdims=True)
        pivot = jnp.sqrt(jnp.sum(jnp.where(index == outer, value, 0.0), axis=0, keepdims=True))
        column = jnp.where(index >= outer, value / pivot, 0.0)
        row = jnp.sum(jnp.where(diagonal, column, 0.0), axis=0, keepdims=True)
        tile = tile - column * row
        columns.append(column)
        pivots.append(pivot)
    accum = -jnp.sum(jnp.where(diagonal, rhs, 0.0), axis=1, keepdims=True)
    middle = jnp.zeros_like(accum)
    for outer in range(size):
        value = jnp.sum(jnp.where(index == outer, accum, 0.0), axis=0, keepdims=True) / pivots[outer]
        middle = jnp.where(index == outer, value, middle)
        accum = accum - columns[outer] * value
    result = jnp.zeros_like(middle)
    for outer in range(size - 1, -1, -1):
        below = jnp.sum(jnp.where(index > outer, columns[outer] * result, 0.0), axis=0, keepdims=True)
        value = jnp.sum(jnp.where(index == outer, middle, 0.0), axis=0, keepdims=True)
        result = jnp.where(index == outer, (value - below) / pivots[outer], result)
    out_ref[...] = jnp.sum(jnp.where(diagonal, result, 0.0), axis=0, keepdims=True)[:, :size]


def assembly_kernel(jacobian_ref, along_ref, cross_ref, scalar_ref, out_ref, deflator_ref, *, total):
    scalars = scalar_ref[...]
    gap_sum = scalars[:, 0:1]
    mismatch_sum = scalars[:, 1:2]
    distance = gap_sum / total + SMALL_EPSILON
    deflator = 1.0 / distance + 1.0
    slopes_row = -2.0 * (along_ref[...] / total) / (distance * distance)
    cross_row = cross_ref[...]
    tile = jacobian_ref[...]
    rows = lax.broadcasted_iota(jnp.int32, tile.shape, 0)
    cols = lax.broadcasted_iota(jnp.int32, tile.shape, 1)
    diagonal = rows == cols
    slopes_col = jnp.sum(jnp.where(diagonal, slopes_row, 0.0), axis=1, keepdims=True)
    cross_col = jnp.sum(jnp.where(diagonal, cross_row, 0.0), axis=1, keepdims=True)
    gram = (
        deflator * deflator * tile
        + deflator * slopes_col * cross_row
        + deflator * cross_col * slopes_row
        + slopes_col * slopes_row * mismatch_sum
    ) / total
    rhs = (deflator * deflator * cross_row + deflator * slopes_row * mismatch_sum) / total
    cholesky_kernel(gram, rhs, out_ref)
    deflator_ref[...] = deflator


def solve_small(jacobian_sum, along_sum, cross_sum, scalars, total):
    size = jacobian_sum.shape[0]
    return pl.pallas_call(
        functools.partial(assembly_kernel, total=total),
        out_shape=(
            jax.ShapeDtypeStruct((1, size), jnp.float32),
            jax.ShapeDtypeStruct((1, 1), jnp.float32),
        ),
    )(jacobian_sum, along_sum.reshape(1, size), cross_sum.reshape(1, size), scalars.reshape(1, 2))


def on_device(state, panel, region, feed_table, step_counts):
    start = state[0, 0]
    row_count = start.shape[1]
    column_count = start.shape[2]
    directions = panel.shape[2]
    tangent = panel[0, 0].reshape(2 * directions, row_count, column_count)
    stacked = jnp.concatenate([start, tangent], 0)
    following = passed_along(stacked, "tm", -1)
    partner_state = swapped(start, "branch", 0)
    classes = jnp.arange(feed_table.shape[0], dtype=jnp.int32)
    feed_rate = jnp.sum(
        jnp.where(region[None] == classes[:, None, None], feed_table[:, None, None], 0.0), 0
    )
    step_limit = step_counts[0]
    panel_rows = panel[0, 0].reshape(directions, -1)
    gap = (start - partner_state).reshape(-1)
    total = 2.0 * lax.axis_size("tm") * row_count * lax.axis_size(SPACE) * column_count
    gap_part = jnp.sum(gap * gap)
    along_part = jnp.sum(panel_rows * gap[None, :], 1)
    count = lax.axis_size(SPACE)
    pieces = (start, tangent, feed_rate[None])
    head = jnp.concatenate([piece[:, :STEPS] for piece in pieces], 0)
    tail = jnp.concatenate([piece[:, -STEPS:] for piece in pieces], 0)
    before = lax.ppermute(tail, SPACE, [(i, (i + 1) % count) for i in range(count)])
    after = lax.ppermute(head, SPACE, [((i + 1) % count, i) for i in range(count)])

    def wide(index, interior):
        return jnp.concatenate([before[index], interior, after[index]], -2)

    fields = (
        wide(0, start[0]),
        wide(1, start[1]),
        wide(slice(2, -1, 2), tangent[0::2]),
        wide(slice(3, -1, 2), tangent[1::2]),
    )
    feed_wide = wide(-1, feed_rate)
    total_rows = feed_wide.shape[0]
    for step_index in range(STEPS):
        fields = advance(
            fields,
            feed_wide[step_index + 1 : total_rows - step_index - 1],
            step_index < step_limit,
        )
    end_state = jnp.stack(fields[:2], 0)
    end_tangent = jnp.stack(fields[2:], 1).reshape(directions, -1)
    arrived = passed_along(end_state, "tm", 1)
    next_mismatch = (end_state - following[:2]).reshape(-1)
    next_jacobian = end_tangent - following[2:].reshape(directions, -1)
    jacobian_gram = jnp.dot(next_jacobian, next_jacobian.T, precision=HIGH)
    jacobian_mismatch = jnp.sum(next_jacobian * next_mismatch[None, :], 1)
    mismatch_square = jnp.sum(next_mismatch * next_mismatch)
    moments = one_axis_at_a_time(
        jnp.concatenate(
            [
                gap_part[None],
                mismatch_square[None],
                along_part,
                jacobian_mismatch,
                jacobian_gram.reshape(-1),
            ]
        ),
        TM_SPACE,
    )
    scalars = moments[:2]
    along_sum = moments[2 : 2 + directions]
    cross_sum = moments[2 + directions : 2 + 2 * directions]
    jacobian_sum = moments[2 + 2 * directions :].reshape(directions, directions)
    coefficients, deflator = solve_small(jacobian_sum, along_sum, cross_sum, scalars, total)
    mismatch = (arrived - start).reshape(-1)
    deflated = deflator.reshape(()) * mismatch
    correction = jnp.sum(coefficients.reshape(directions, 1, 1, 1) * panel[0, 0], 0)
    return (
        deflated.reshape(1, 1, 2, row_count, column_count),
        correction.reshape(1, 1, 2, row_count, column_count),
        coefficients.reshape(1, directions),
    )


def solution(mesh):
    finer = Mesh(
        mesh.devices.reshape(mesh.shape["tm"], 4, 4, mesh.shape["branch"]),
        ("tm", "space_0", "space_1", "branch"),
    )
    in_specs = (
        P("branch", "tm", None, SPACE, None),
        P("branch", "tm", None, None, SPACE, None),
        P(SPACE, None),
        P(),
        P("tm"),
    )
    out_specs = (
        P("branch", "tm", None, SPACE, None),
        P("branch", "tm", None, SPACE, None),
        P("branch", None),
    )
    return jax.shard_map(
        on_device, mesh=finer, in_specs=in_specs, out_specs=out_specs, check_vma=False
    )
```
